32 devices in a mesh: depth: 8 (over z, x), tile: 4 (over y, core).
Axes of the slice: x: 2, y: 2, z: 4, core: 2. Of those that a mesh axis runs over, the one named last changes fastest.
Arguments:
- hologram: bfloat16 [2, 256, 4096], P(None, 'tile'), may hold values from -6 to 6
- kernel: bfloat16 [32, 2, 64], P('depth'), may hold values from -0.5 to 0.5
- depth_prior: float32 [32, 256], P('depth', 'tile'), may hold values from -6 to 320
Outputs:
- plane_stack: float32 [32, 256, 4096], P('depth', 'tile')
- joined_intensity: float32 [256, 4096], P('tile', 'depth')
- mean_depth: float32 [256, 4096], P('tile', 'depth')
The draws below stay inside these ranges and needn't reach their ends.
All inputs are finite; a program needn't handle non-finite values.
Results may differ from the reference program's by a relative error of at most 0.0031.
Values may be sent and summed in bfloat16 or wider, within the bound.
No kernel may reach another device: no remote copies, remote signals or barrier semaphores. Data moves between devices by JAX's collectives and lax.ppermute only.
A program may use at most 128 MiB of HBM per device.

```python
import jax
import jax.numpy as jnp
from jax import lax

NC = 4096
TAPS = 64
NR = 256
PLANES = 32


def draw_depth_prior(key, part):
    noise_key = jax.random.fold_in(key, 0)
    spread = jnp.clip(1.5 * jax.random.normal(noise_key, (PLANES, NR), jnp.float32), -6.0, 6.0)
    return spread


def block_scale(own_key, shape, pieces, least, high):
    factor_of, own = 1.0, jax.random.fold_in(own_key, 6)
    for axis_at, parts in pieces:
        steps = jnp.exp(jax.random.uniform(jax.random.fold_in(own, axis_at), (parts,), jnp.float32, least / len(pieces), high / len(pieces)))
        factor_of = factor_of * jnp.repeat(steps, shape[axis_at] // parts).reshape([-1 if axis == axis_at else 1 for axis in range(len(shape))])
    return factor_of


def centred(own_key, dims, scale, reach, pieces=(), kind=jnp.bfloat16):
    entries = jax.random.normal(own_key, dims, jnp.float32) * scale
    if len(pieces) > 0:
        entries = block_scale(own_key, dims, pieces, -0.22, 0.18) * entries
    return jnp.clip(entries, min=-reach, max=reach).astype(kind)


def setup_inputs(seed: int = 0) -> dict:
    arg_keys = jax.random.split(jax.random.key(seed), 4)
    hologram = centred(arg_keys[0], (2, NR, NC), 1.0, 6.0, ((1, 4),))
    kernel = centred(arg_keys[1], (PLANES, 2, TAPS), (2 * TAPS) ** -0.5, 0.5, ((0, 8),))
    depth_prior = draw_depth_prior(jax.random.fold_in(arg_keys[3], 71), 0)
    return {"hologram": hologram, "kernel": kernel, "depth_prior": depth_prior}


def correlate(spectrum, length, taps_re, taps_im, along):
    flipped = lax.complex(taps_re[::-1], taps_im[::-1])
    kernel_spec = jnp.fft.fft(flipped, n=length + TAPS)
    if along == 0:
        kernel_spec = kernel_spec[:, None]
    else:
        kernel_spec = kernel_spec[None, :]
    convolved = jnp.fft.ifft(spectrum * kernel_spec, axis=along)
    offset = TAPS - 1 - TAPS // 2
    return lax.slice_in_dim(convolved, offset, offset + length, axis=along)


def sharpness(intensity):
    padded = jnp.pad(intensity, 1)
    vertical = padded[:-2] + 2.0 * padded[1:-1] + padded[2:]
    grad_x = vertical[:, 2:] - vertical[:, :-2]
    horizontal = padded[:, :-2] + 2.0 * padded[:, 1:-1] + padded[:, 2:]
    grad_y = horizontal[2:] - horizontal[:-2]
    return grad_x * grad_x + grad_y * grad_y


def reference(hologram, kernel, depth_prior):
    signal = hologram.astype(jnp.float32)
    spectrum = jnp.fft.fft(lax.complex(signal[0], signal[1]), n=NR + TAPS, axis=0)
    plane_taps = kernel.astype(jnp.float32)
    depth_values = (jnp.arange(PLANES, dtype=jnp.float32) + 0.5) / PLANES

    def one_plane(running, inputs):
        taps_pair, prior_row, depth_value = inputs
        across = correlate(spectrum, NR, taps_pair[0], taps_pair[1], 0)
        across_re = lax.optimization_barrier(jnp.real(across).astype(jnp.bfloat16)).astype(jnp.float32)
        across_im = lax.optimization_barrier(jnp.imag(across).astype(jnp.bfloat16)).astype(jnp.float32)
        col_spectrum = jnp.fft.fft(lax.complex(across_re, across_im), n=NC + TAPS, axis=1)
        field = correlate(col_spectrum, NC, taps_pair[0], taps_pair[1], 1)
        field_re = jnp.real(field)
        field_im = jnp.imag(field)
        intensity = field_re * field_re + field_im * field_im
        score = prior_row[:, None] + jnp.log(1.0 + sharpness(intensity))
        peak_now, weight_sum, weighted, placed = running
        peak_next = jnp.maximum(peak_now, score)
        factor = jnp.exp(peak_now - peak_next)
        fresh_term = jnp.exp(score - peak_next)
        running = (peak_next, weight_sum * factor + fresh_term, weighted * factor + fresh_term * intensity, placed * factor + fresh_term * depth_value)
        return running, intensity

    start_peak = jnp.full((NR, NC), -jnp.inf, dtype=jnp.float32)
    zeros_map = jnp.zeros((NR, NC), dtype=jnp.float32)
    running, plane_stack = lax.scan(one_plane, (start_peak, zeros_map, zeros_map, zeros_map), (plane_taps, depth_prior, depth_values))
    return plane_stack, running[2] / running[1], running[3] / running[1]
```

```python
import jax
import jax.numpy as jnp
from jax import lax
from jax.sharding import PartitionSpec as P

TAPS = 64
LANE = 128


def skewed(taps, n_out, n_in):
    count = taps.shape[0]
    row = jnp.pad(taps, ((0, 0), (0, n_in + 1 - TAPS)))
    flat = jnp.tile(row, (1, n_out))[:, : n_out * n_in]
    return flat.reshape(count, n_out, n_in)


def rows_matrix(taps_re, taps_im, n_out, n_in):
    base_re = skewed(taps_re, n_out, n_in)
    base_im = skewed(taps_im, n_out, n_in)
    upper_half = jnp.concatenate([base_re, -base_im], axis=2)
    lower_half = jnp.concatenate([base_im, base_re], axis=2)
    return jnp.concatenate([upper_half, lower_half], axis=1)


def propagate_rows(window, taps_re, taps_im, n_out):
    n_in = window.shape[1]
    matrix = rows_matrix(taps_re, taps_im, n_out, n_in)
    stacked = window.reshape(2 * n_in, window.shape[2])
    product = jnp.einsum("pji,ic->pjc", matrix, stacked, preferred_element_type=jnp.float32)
    across = product.astype(jnp.bfloat16)
    return across[:, :n_out], across[:, n_out:]


def propagate_columns(across_re, across_im, taps_re, taps_im):
    count, row_total, width = across_re.shape
    block_count = width // LANE - 1

    def windows(signal):
        tiles = signal.reshape(count, row_total, block_count + 1, LANE)
        return jnp.concatenate([tiles[:, :, :block_count], tiles[:, :, 1:, :TAPS]], axis=3)

    stacked = jnp.concatenate([windows(across_re), windows(across_im)], axis=3)
    base_re = skewed(taps_re, LANE, LANE + TAPS)
    base_im = skewed(taps_im, LANE, LANE + TAPS)
    upper_half = jnp.concatenate([base_re, base_im], axis=1)
    lower_half = jnp.concatenate([-base_im, base_re], axis=1)
    matrix = jnp.concatenate([upper_half, lower_half], axis=2)
    product = jnp.einsum("prbi,pji->prbj", stacked, matrix, preferred_element_type=jnp.float32)
    field_re = product[..., :LANE].reshape(count, row_total, block_count * LANE)
    field_im = product[..., LANE:].reshape(count, row_total, block_count * LANE)
    return field_re, field_im


def sharpness(rimmed):
    vertical = rimmed[:, :-2] + 2.0 * rimmed[:, 1:-1] + rimmed[:, 2:]
    grad_x = vertical[:, :, 2:] - vertical[:, :, :-2]
    horizontal = rimmed[:, :, :-2] + 2.0 * rimmed[:, :, 1:-1] + rimmed[:, :, 2:]
    grad_y = horizontal[:, 2:] - horizontal[:, :-2]
    return grad_x * grad_x + grad_y * grad_y


def local(hologram, kernel, depth_prior):
    _, rows, col_total = hologram.shape
    local_planes = kernel.shape[0]
    depth_count = lax.axis_size("depth")
    tile_count = lax.axis_size("tile")
    depth_at = lax.axis_index("depth")
    tile_at = lax.axis_index("tile")
    planes_total = local_planes * depth_count
    own_cols = col_total // depth_count
    row_total = rows * tile_count
    half_taps = TAPS // 2

    packed = jnp.concatenate(
        [kernel.reshape(local_planes, 2 * TAPS).astype(jnp.float32), depth_prior], axis=1
    )
    packed_all = lax.all_gather(packed, "depth", tiled=True)
    taps_all = packed_all[:, : 2 * TAPS].astype(jnp.bfloat16).reshape(planes_total, 2, TAPS)
    prior_all = packed_all[:, 2 * TAPS :]

    above_rows, below_rows = 48, 32
    above = lax.ppermute(
        hologram[:, rows - above_rows :], "tile", [(i, i + 1) for i in range(tile_count - 1)]
    )
    below = lax.ppermute(
        hologram[:, :below_rows], "tile", [(i + 1, i) for i in range(tile_count - 1)]
    )
    extended = jnp.concatenate([above, hologram, below], axis=1)

    window = extended[:, above_rows - half_taps : above_rows - half_taps + rows + TAPS]
    across_re, across_im = propagate_rows(window, kernel[:, 0], kernel[:, 1], rows)
    pad_cols = ((0, 0), (0, 0), (half_taps, LANE - half_taps))
    field_re, field_im = propagate_columns(
        jnp.pad(across_re, pad_cols), jnp.pad(across_im, pad_cols), kernel[:, 0], kernel[:, 1]
    )
    plane_stack = field_re * field_re + field_im * field_im

    rim_rows = rows + 2
    window = extended[:, above_rows - half_taps - 1 : above_rows - half_taps - 1 + rim_rows + TAPS - 1]
    lead = LANE // 2 + half_taps
    width = own_cols + 2 * LANE
    window = jnp.pad(window, ((0, 0), (0, 0), (lead, width - lead)))
    window = lax.dynamic_slice_in_dim(window, depth_at * own_cols, width, axis=2)
    across_re, across_im = propagate_rows(window, taps_all[:, 0], taps_all[:, 1], rim_rows)
    field_re, field_im = propagate_columns(across_re, across_im, taps_all[:, 0], taps_all[:, 1])
    start = LANE // 2 - 1
    field_re = field_re[:, :, start : start + own_cols + 2]
    field_im = field_im[:, :, start : start + own_cols + 2]
    rimmed = field_re * field_re + field_im * field_im
    row_at = tile_at * rows - 1 + jnp.arange(rim_rows)
    col_at = depth_at * own_cols - 1 + jnp.arange(own_cols + 2)
    inside = ((row_at >= 0) & (row_at < row_total))[:, None] & (
        (col_at >= 0) & (col_at < col_total)
    )[None, :]
    rimmed = jnp.where(inside[None], rimmed, 0.0)
    score = prior_all[:, :, None] + jnp.log(1.0 + sharpness(rimmed))
    intensity = rimmed[:, 1:-1, 1:-1]
    peak = jnp.max(score, axis=0)
    fresh = jnp.exp(score - peak[None])
    depth_values = (jnp.arange(planes_total, dtype=jnp.float32) + 0.5) / planes_total
    weight_sum = jnp.sum(fresh, axis=0)
    weighted = jnp.sum(fresh * intensity, axis=0)
    placed = jnp.sum(fresh * depth_values[:, None, None], axis=0)
    return (plane_stack, weighted / weight_sum, placed / weight_sum)


def solution(mesh):
    in_specs = (P(None, "tile", None), P("depth", None, None), P("depth", "tile"))
    out_specs = (P("depth", "tile", None), P("tile", "depth"), P("tile", "depth"))
    return jax.shard_map(local, mesh=mesh, in_specs=in_specs, out_specs=out_specs, check_vma=False)
```

```python
import functools

import jax
import jax.numpy as jnp
from jax import lax
from jax.experimental import pallas as pl
from jax.experimental.pallas import tpu as pltpu
from jax.sharding import PartitionSpec as P

TAPS = 64
LANE = 128
SPAN = 2 * LANE


def propagate_kernel(taps_ref, window_ref, out_ref, *, n_out, n_in, block_count):
    def skew(taps):
        return pltpu.roll(jnp.broadcast_to(taps, (LANE, SPAN)), 0, 1, stride=1, stride_axis=0)

    skew_re = skew(taps_ref[0, 0:1, :])
    skew_im = skew(taps_ref[0, 1:2, :])
    rows_re = skew_re[:n_out, :n_in]
    rows_im = skew_im[:n_out, :n_in]
    rows_matrix = jnp.concatenate(
        [
            jnp.concatenate([rows_re, -rows_im], axis=1),
            jnp.concatenate([rows_im, rows_re], axis=1),
        ],
        axis=0,
    ).astype(jnp.bfloat16)
    across = jnp.dot(rows_matrix, window_ref[...], preferred_element_type=jnp.float32)
    across = across.astype(jnp.bfloat16)
    across_re = across[:n_out]
    across_im = across[n_out:]

    def stacked(signal, first):
        return jnp.concatenate(
            [signal[:, LANE * b : LANE * (b + 1)] for b in range(first, first + block_count)], axis=0
        )

    blocks = jnp.concatenate(
        [stacked(across_re, 0), stacked(across_re, 1), stacked(across_im, 0), stacked(across_im, 1)],
        axis=1,
    )
    near_re = skew_re[:, :LANE].T
    far_re = skew_re[:, LANE:].T
    near_im = skew_im[:, :LANE].T
    far_im = skew_im[:, LANE:].T
    cols_matrix = jnp.concatenate(
        [
            jnp.concatenate([near_re, near_im], axis=1),
            jnp.concatenate([far_re, far_im], axis=1),
            jnp.concatenate([-near_im, near_re], axis=1),
            jnp.concatenate([-far_im, far_re], axis=1),
        ],
        axis=0,
    ).astype(jnp.bfloat16)
    field = jnp.dot(blocks, cols_matrix, preferred_element_type=jnp.float32)
    intensity = field[:, :LANE] * field[:, :LANE] + field[:, LANE:] * field[:, LANE:]
    for b in range(block_count):
        out_ref[0, :, LANE * b : LANE * (b + 1)] = intensity[n_out * b : n_out * (b + 1)]


def propagate(taps, window, n_out):
    planes = taps.shape[0]
    _, n_in, width = window.shape
    block_count = width // LANE - 1
    stacked = window.reshape(2 * n_in, width)
    body = functools.partial(
        propagate_kernel, n_out=n_out, n_in=n_in, block_count=block_count
    )
    flops = 2 * planes * (2 * n_out * 2 * n_in * width + block_count * n_out * 4 * LANE * SPAN)
    return pl.pallas_call(
        body,
        grid=(planes,),
        in_specs=[
            pl.BlockSpec((1, 2, SPAN), lambda p: (p, 0, 0)),
            pl.BlockSpec((2 * n_in, width), lambda p: (0, 0)),
        ],
        out_specs=pl.BlockSpec((1, n_out, block_count * LANE), lambda p: (p, 0, 0)),
        out_shape=jax.ShapeDtypeStruct((planes, n_out, block_count * LANE), jnp.float32),
        cost_estimate=pl.CostEstimate(
            flops=flops,
            transcendentals=0,
            bytes_accessed=stacked.size * 2 + planes * n_out * block_count * LANE * 4,
        ),
    )(taps, stacked)


def gather_depth(block):
    count = lax.axis_size("depth")
    have = 1
    while have < count:
        need = min(have, count - have)
        moved = lax.ppermute(
            block[: need * (block.shape[0] // have)],
            "depth",
            [((j + have) % count, j) for j in range(count)],
        )
        block = jnp.concatenate([block, moved], axis=0)
        have += need
    return block


def sharpness(rimmed):
    vertical = rimmed[:, :-2] + 2.0 * rimmed[:, 1:-1] + rimmed[:, 2:]
    grad_x = vertical[:, :, 2:] - vertical[:, :, :-2]
    horizontal = rimmed[:, :, :-2] + 2.0 * rimmed[:, :, 1:-1] + rimmed[:, :, 2:]
    grad_y = horizontal[:, 2:] - horizontal[:, :-2]
    return grad_x * grad_x + grad_y * grad_y


def local(hologram, kernel, depth_prior):
    _, rows, col_total = hologram.shape
    local_planes = kernel.shape[0]
    depth_count = lax.axis_size("depth")
    tile_count = lax.axis_size("tile")
    depth_at = lax.axis_index("depth")
    tile_at = lax.axis_index("tile")
    planes_total = local_planes * depth_count
    own_cols = col_total // depth_count
    row_total = rows * tile_count
    half_taps = TAPS // 2

    taps = jnp.pad(kernel.astype(jnp.float32), ((0, 0), (0, 0), (0, SPAN - TAPS)))
    packed = jnp.concatenate([taps.reshape(local_planes, 2 * SPAN), depth_prior], axis=1)
    packed_all = gather_depth(packed)
    taps_all = packed_all[:, : 2 * SPAN].reshape(planes_total, 2, SPAN)
    prior_all = packed_all[:, 2 * SPAN :]
    owner = (depth_at + jnp.arange(planes_total) // local_planes) % depth_count
    plane_at = owner * local_planes + jnp.arange(planes_total) % local_planes

    halo = 48
    above = lax.ppermute(
        hologram[:, rows - halo :], "tile", [(i, i + 1) for i in range(tile_count - 1)]
    )
    below = lax.ppermute(hologram[:, :halo], "tile", [(i + 1, i) for i in range(tile_count - 1)])
    extended = jnp.concatenate([above, hologram, below], axis=1)

    window = extended[:, halo - half_taps : halo - half_taps + LANE]
    window = jnp.pad(window, ((0, 0), (0, 0), (half_taps, LANE - half_taps)))
    plane_stack = propagate(taps, window, rows)

    lead_rows = 8
    n_out = rows + 2 * lead_rows
    first = halo - half_taps - lead_rows
    window = extended[:, first : first + n_out + TAPS - 1]
    lead = LANE // 2 + half_taps
    width = own_cols + 2 * LANE
    window = jnp.pad(
        window, ((0, 0), (0, SPAN - window.shape[1]), (lead, width - lead))
    )
    window = lax.dynamic_slice_in_dim(window, depth_at * own_cols, width, axis=2)
    field = propagate(taps_all, window, n_out)
    start = LANE // 2 - 1
    rimmed = field[:, lead_rows - 1 : lead_rows + rows + 1, start : start + own_cols + 2]
    row_at = tile_at * rows - 1 + jnp.arange(rows + 2)
    col_at = depth_at * own_cols - 1 + jnp.arange(own_cols + 2)
    inside = ((row_at >= 0) & (row_at < row_total))[:, None] & (
        (col_at >= 0) & (col_at < col_total)
    )[None, :]
    rimmed = jnp.where(inside[None], rimmed, 0.0)
    score = prior_all[:, :, None] + jnp.log(1.0 + sharpness(rimmed))
    intensity = rimmed[:, 1:-1, 1:-1]
    peak = jnp.max(score, axis=0)
    fresh = jnp.exp(score - peak[None])
    depth_values = (plane_at.astype(jnp.float32) + 0.5) / planes_total
    weight_sum = jnp.sum(fresh, axis=0)
    weighted = jnp.sum(fresh * intensity, axis=0)
    placed = jnp.sum(fresh * depth_values[:, None, None], axis=0)
    return (plane_stack, weighted / weight_sum, placed / weight_sum)


def solution(mesh):
    in_specs = (P(None, "tile", None), P("depth", None, None), P("depth", "tile"))
    out_specs = (P("depth", "tile", None), P("tile", "depth"), P("tile", "depth"))
    return jax.shard_map(local, mesh=mesh, in_specs=in_specs, out_specs=out_specs, check_vma=False)
```

```python
import functools

import jax
import jax.numpy as jnp
from jax import lax
from jax.experimental import pallas as pl
from jax.experimental.pallas import tpu as pltpu
from jax.sharding import PartitionSpec as P

TAPS = 64
LANE = 128
SPAN = 2 * LANE


def stacked_intensity(taps_ref, window_ref, n_out, n_in, block_count):
    def skew(taps):
        return pltpu.roll(jnp.broadcast_to(taps, (LANE, SPAN)), 0, 1, stride=1, stride_axis=0)

    skew_re = skew(taps_ref[0, 0:1, :])
    skew_im = skew(taps_ref[0, 1:2, :])
    rows_re = skew_re[:n_out, :n_in]
    rows_im = skew_im[:n_out, :n_in]
    rows_matrix = jnp.concatenate(
        [
            jnp.concatenate([rows_re, -rows_im], axis=1),
            jnp.concatenate([rows_im, rows_re], axis=1),
        ],
        axis=0,
    ).astype(jnp.bfloat16)
    across = jnp.dot(rows_matrix, window_ref[...], preferred_element_type=jnp.float32)
    across = across.astype(jnp.bfloat16)
    across_re = across[:n_out]
    across_im = across[n_out:]

    def stacked(signal, first):
        return jnp.concatenate(
            [signal[:, LANE * b : LANE * (b + 1)] for b in range(first, first + block_count)], axis=0
        )

    blocks = jnp.concatenate(
        [stacked(across_re, 0), stacked(across_re, 1), stacked(across_im, 0), stacked(across_im, 1)],
        axis=1,
    )
    near_re = skew_re[:, :LANE].T
    far_re = skew_re[:, LANE:].T
    near_im = skew_im[:, :LANE].T
    far_im = skew_im[:, LANE:].T
    cols_matrix = jnp.concatenate(
        [
            jnp.concatenate([near_re, near_im], axis=1),
            jnp.concatenate([far_re, far_im], axis=1),
            jnp.concatenate([-near_im, near_re], axis=1),
            jnp.concatenate([-far_im, far_re], axis=1),
        ],
        axis=0,
    ).astype(jnp.bfloat16)
    field = jnp.dot(blocks, cols_matrix, preferred_element_type=jnp.float32)
    return field[:, :LANE] * field[:, :LANE] + field[:, LANE:] * field[:, LANE:]


def propagate_kernel(taps_ref, window_ref, out_ref, *, n_out, n_in, block_count):
    intensity = stacked_intensity(taps_ref, window_ref, n_out, n_in, block_count)
    for b in range(block_count):
        out_ref[0, :, LANE * b : LANE * (b + 1)] = intensity[n_out * b : n_out * (b + 1)]


def joining_kernel(
    corner_ref, taps_ref, prior_ref, depth_ref, window_ref, joined_ref, mean_ref,
    peak_ref, total_ref, weighted_ref, placed_ref, *, n_out, n_in, block_count, bounds,
):
    plane = pl.program_id(0)
    stacked = stacked_intensity(taps_ref, window_ref, n_out, n_in, block_count)
    intensity = jnp.concatenate(
        [stacked[n_out * b : n_out * (b + 1)] for b in range(block_count)], axis=1
    )
    height, width = intensity.shape
    row_at = corner_ref[0] + lax.broadcasted_iota(jnp.int32, (height, width), 0)
    col_at = corner_ref[1] + lax.broadcasted_iota(jnp.int32, (height, width), 1)
    inside = (row_at >= 0) & (row_at < bounds[0]) & (col_at >= 0) & (col_at < bounds[1])
    intensity = jnp.where(inside, intensity, 0.0)
    vertical = (
        pltpu.roll(intensity, 1, 0) + 2.0 * intensity + pltpu.roll(intensity, height - 1, 0)
    )
    grad_x = pltpu.roll(vertical, width - 1, 1) - pltpu.roll(vertical, 1, 1)
    horizontal = (
        pltpu.roll(intensity, 1, 1) + 2.0 * intensity + pltpu.roll(intensity, width - 1, 1)
    )
    grad_y = pltpu.roll(horizontal, height - 1, 0) - pltpu.roll(horizontal, 1, 0)
    score = prior_ref[0] + jnp.log(1.0 + (grad_x * grad_x + grad_y * grad_y))
    depth_value = depth_ref[0]

    @pl.when(plane == 0)
    def _():
        peak_ref[...] = score
        total_ref[...] = jnp.ones_like(score)
        weighted_ref[...] = intensity
        placed_ref[...] = jnp.broadcast_to(depth_value, score.shape)

    @pl.when(plane > 0)
    def _():
        peak_now = peak_ref[...]
        peak_next = jnp.maximum(peak_now, score)
        factor = jnp.exp(peak_now - peak_next)
        fresh = jnp.exp(score - peak_next)
        peak_ref[...] = peak_next
        total_ref[...] = total_ref[...] * factor + fresh
        weighted_ref[...] = weighted_ref[...] * factor + fresh * intensity
        placed_ref[...] = placed_ref[...] * factor + fresh * depth_value

    @pl.when(plane == pl.num_programs(0) - 1)
    def _():
        joined_ref[...] = weighted_ref[...] / total_ref[...]
        mean_ref[...] = placed_ref[...] / total_ref[...]


def propagate(taps, window, n_out):
    planes = taps.shape[0]
    _, n_in, width = window.shape
    block_count = width // LANE - 1
    stacked = window.reshape(2 * n_in, width)
    body = functools.partial(
        propagate_kernel, n_out=n_out, n_in=n_in, block_count=block_count
    )
    flops = 2 * planes * (2 * n_out * 2 * n_in * width + block_count * n_out * 4 * LANE * SPAN)
    return pl.pallas_call(
        body,
        grid=(planes,),
        in_specs=[
            pl.BlockSpec((1, 2, SPAN), lambda p: (p, 0, 0)),
            pl.BlockSpec((2 * n_in, width), lambda p: (0, 0)),
        ],
        out_specs=pl.BlockSpec((1, n_out, block_count * LANE), lambda p: (p, 0, 0)),
        out_shape=jax.ShapeDtypeStruct((planes, n_out, block_count * LANE), jnp.float32),
        cost_estimate=pl.CostEstimate(
            flops=flops,
            transcendentals=0,
            bytes_accessed=stacked.size * 2 + planes * n_out * block_count * LANE * 4,
        ),
    )(taps, stacked)


def joining(corner, taps, prior, depth_values, window, n_out, bounds):
    planes = taps.shape[0]
    _, n_in, width = window.shape
    block_count = width // LANE - 1
    stacked = window.reshape(2 * n_in, width)
    body = functools.partial(
        joining_kernel, n_out=n_out, n_in=n_in, block_count=block_count, bounds=bounds
    )
    out_cols = block_count * LANE
    flops = 2 * planes * (2 * n_out * 2 * n_in * width + block_count * n_out * 4 * LANE * SPAN)
    grid_spec = pltpu.PrefetchScalarGridSpec(
        num_scalar_prefetch=1,
        grid=(planes,),
        in_specs=[
            pl.BlockSpec((1, 2, SPAN), lambda p, c: (p, 0, 0)),
            pl.BlockSpec((1, n_out, 1), lambda p, c: (p, 0, 0)),
            pl.BlockSpec((1, 1, 1), lambda p, c: (p, 0, 0)),
            pl.BlockSpec((2 * n_in, width), lambda p, c: (0, 0)),
        ],
        out_specs=[
            pl.BlockSpec((n_out, out_cols), lambda p, c: (0, 0)),
            pl.BlockSpec((n_out, out_cols), lambda p, c: (0, 0)),
        ],
        scratch_shapes=[pltpu.VMEM((n_out, out_cols), jnp.float32) for _ in range(4)],
    )
    return pl.pallas_call(
        body,
        grid_spec=grid_spec,
        out_shape=[jax.ShapeDtypeStruct((n_out, out_cols), jnp.float32)] * 2,
        compiler_params=pltpu.CompilerParams(dimension_semantics=("arbitrary",)),
        cost_estimate=pl.CostEstimate(
            flops=flops,
            transcendentals=3 * planes * n_out * out_cols,
            bytes_accessed=stacked.size * 2 + 2 * n_out * out_cols * 4,
        ),
    )(corner, taps, prior, depth_values, stacked)


def gather_depth(block):
    count = lax.axis_size("depth")
    moved = [
        lax.ppermute(block, "depth", [((j + shift) % count, j) for j in range(count)])
        for shift in range(1, count)
    ]
    return jnp.concatenate([block, *moved], axis=0)


def local(hologram, kernel, depth_prior):
    _, rows, col_total = hologram.shape
    local_planes = kernel.shape[0]
    depth_count = lax.axis_size("depth")
    tile_count = lax.axis_size("tile")
    depth_at = lax.axis_index("depth")
    tile_at = lax.axis_index("tile")
    planes_total = local_planes * depth_count
    own_cols = col_total // depth_count
    row_total = rows * tile_count
    half_taps = TAPS // 2

    taps = jnp.pad(kernel.astype(jnp.float32), ((0, 0), (0, 0), (0, SPAN - TAPS)))
    packed = jnp.concatenate([taps.reshape(local_planes, 2 * SPAN), depth_prior], axis=1)
    packed_all = gather_depth(packed)
    owner = (depth_at + jnp.arange(planes_total) // local_planes) % depth_count
    plane_at = owner * local_planes + jnp.arange(planes_total) % local_planes

    halo = 48
    above = lax.ppermute(
        hologram[:, rows - halo :], "tile", [(i, i + 1) for i in range(tile_count - 1)]
    )
    below = lax.ppermute(hologram[:, :halo], "tile", [(i + 1, i) for i in range(tile_count - 1)])
    extended = jnp.concatenate([above, hologram, below], axis=1)

    window = extended[:, halo - half_taps : halo - half_taps + LANE]
    window = jnp.pad(window, ((0, 0), (0, 0), (half_taps, LANE - half_taps)))
    plane_stack = propagate(taps, window, rows)
    plane_stack, packed_all = lax.optimization_barrier((plane_stack, packed_all))
    taps_all = packed_all[:, : 2 * SPAN].reshape(planes_total, 2, SPAN)
    prior_all = packed_all[:, 2 * SPAN :]

    lead_rows = 8
    n_out = rows + 2 * lead_rows
    first = halo - half_taps - lead_rows
    window = extended[:, first : first + n_out + TAPS - 1]
    lead = LANE // 2 + half_taps
    width = own_cols + 2 * LANE
    window = jnp.pad(
        window, ((0, 0), (0, SPAN - window.shape[1]), (lead, width - lead))
    )
    window = lax.dynamic_slice_in_dim(window, depth_at * own_cols, width, axis=2)
    corner = jnp.stack([tile_at * rows - lead_rows, depth_at * own_cols - LANE // 2]).astype(
        jnp.int32
    )
    prior_rows = jnp.pad(prior_all, ((0, 0), (lead_rows, lead_rows)))[:, :, None]
    depth_values = ((plane_at.astype(jnp.float32) + 0.5) / planes_total)[:, None, None]
    joined, mean_depth = joining(
        corner, taps_all, prior_rows, depth_values, window, n_out, (row_total, col_total)
    )
    start = LANE // 2
    joined = joined[lead_rows : lead_rows + rows, start : start + own_cols]
    mean_depth = mean_depth[lead_rows : lead_rows + rows, start : start + own_cols]
    return (plane_stack, joined, mean_depth)


def solution(mesh):
    in_specs = (P(None, "tile", None), P("depth", None, None), P("depth", "tile"))
    out_specs = (P("depth", "tile", None), P("tile", "depth"), P("tile", "depth"))
    return jax.shard_map(local, mesh=mesh, in_specs=in_specs, out_specs=out_specs, check_vma=False)
```

```python
import functools

import jax
import jax.numpy as jnp
from jax import lax
from jax.experimental import pallas as pl
from jax.experimental.pallas import tpu as pltpu
from jax.sharding import PartitionSpec as P

TAPS = 64
LANE = 128
SPAN = 2 * LANE


def skews(taps_ref, plane):
    def skew(taps):
        return pltpu.roll(jnp.broadcast_to(taps, (LANE, SPAN)), 0, 1, stride=1, stride_axis=0)

    return skew(taps_ref[plane, 0:1, :]), skew(taps_ref[plane, 1:2, :])


def rows_matrix(skew_re, skew_im, n_out, n_in):
    rows_re = skew_re[:n_out, :n_in]
    rows_im = skew_im[:n_out, :n_in]
    return jnp.concatenate(
        [
            jnp.concatenate([rows_re, -rows_im], axis=1),
            jnp.concatenate([rows_im, rows_re], axis=1),
        ],
        axis=0,
    ).astype(jnp.bfloat16)


def across_planes(taps_ref, window_ref, n_out, n_in):
    group = taps_ref.shape[0]
    skewed = [skews(taps_ref, g) for g in range(group)]
    matrix = jnp.concatenate([rows_matrix(*sk, n_out, n_in) for sk in skewed], axis=0)
    across = jnp.dot(matrix, window_ref[...], preferred_element_type=jnp.float32)
    return skewed, across.astype(jnp.bfloat16)


def column_intensity(across, skew_re, skew_im, n_out, block_count):
    across_re = across[:n_out]
    across_im = across[n_out:]

    def stacked(signal, first):
        return jnp.concatenate(
            [signal[:, LANE * b : LANE * (b + 1)] for b in range(first, first + block_count)], axis=0
        )

    blocks = jnp.concatenate(
        [stacked(across_re, 0), stacked(across_re, 1), stacked(across_im, 0), stacked(across_im, 1)],
        axis=1,
    )
    near_re = skew_re[:, :LANE].T
    far_re = skew_re[:, LANE:].T
    near_im = skew_im[:, :LANE].T
    far_im = skew_im[:, LANE:].T
    cols_matrix = jnp.concatenate(
        [
            jnp.concatenate([near_re, near_im], axis=1),
            jnp.concatenate([far_re, far_im], axis=1),
            jnp.concatenate([-near_im, near_re], axis=1),
            jnp.concatenate([-far_im, far_re], axis=1),
        ],
        axis=0,
    ).astype(jnp.bfloat16)
    field = jnp.dot(blocks, cols_matrix, preferred_element_type=jnp.float32)
    return field[:, :LANE] * field[:, :LANE] + field[:, LANE:] * field[:, LANE:]


def propagate_kernel(taps_ref, window_ref, out_ref, *, n_out, n_in, block_count):
    skewed, across = across_planes(taps_ref, window_ref, n_out, n_in)
    for g, (skew_re, skew_im) in enumerate(skewed):
        intensity = column_intensity(
            across[2 * n_out * g : 2 * n_out * (g + 1)], skew_re, skew_im, n_out, block_count
        )
        for b in range(block_count):
            out_ref[g, :, LANE * b : LANE * (b + 1)] = intensity[n_out * b : n_out * (b + 1)]


def joining_kernel(
    corner_ref, taps_ref, prior_ref, depth_ref, window_ref, joined_ref, mean_ref,
    peak_ref, total_ref, weighted_ref, placed_ref, *, n_out, n_in, block_count, bounds,
):
    step = pl.program_id(0)

    @pl.when(step == 0)
    def _():
        peak_ref[...] = jnp.full(peak_ref.shape, -jnp.inf, jnp.float32)
        total_ref[...] = jnp.zeros(total_ref.shape, jnp.float32)
        weighted_ref[...] = jnp.zeros(weighted_ref.shape, jnp.float32)
        placed_ref[...] = jnp.zeros(placed_ref.shape, jnp.float32)

    skewed, across = across_planes(taps_ref, window_ref, n_out, n_in)
    height, width = n_out, block_count * LANE
    row_at = corner_ref[0] + lax.broadcasted_iota(jnp.int32, (height, width), 0)
    col_at = corner_ref[1] + lax.broadcasted_iota(jnp.int32, (height, width), 1)
    inside = (row_at >= 0) & (row_at < bounds[0]) & (col_at >= 0) & (col_at < bounds[1])
    for g, (skew_re, skew_im) in enumerate(skewed):
        stacked = column_intensity(
            across[2 * n_out * g : 2 * n_out * (g + 1)], skew_re, skew_im, n_out, block_count
        )
        intensity = jnp.concatenate(
            [stacked[n_out * b : n_out * (b + 1)] for b in range(block_count)], axis=1
        )
        intensity = jnp.where(inside, intensity, 0.0)
        vertical = (
            pltpu.roll(intensity, 1, 0) + 2.0 * intensity + pltpu.roll(intensity, height - 1, 0)
        )
        grad_x = pltpu.roll(vertical, width - 1, 1) - pltpu.roll(vertical, 1, 1)
        horizontal = (
            pltpu.roll(intensity, 1, 1) + 2.0 * intensity + pltpu.roll(intensity, width - 1, 1)
        )
        grad_y = pltpu.roll(horizontal, height - 1, 0) - pltpu.roll(horizontal, 1, 0)
        score = prior_ref[g] + jnp.log(1.0 + (grad_x * grad_x + grad_y * grad_y))
        peak_now = peak_ref[...]
        peak_next = jnp.maximum(peak_now, score)
        factor = jnp.exp(peak_now - peak_next)
        fresh = jnp.exp(score - peak_next)
        peak_ref[...] = peak_next
        total_ref[...] = total_ref[...] * factor + fresh
        weighted_ref[...] = weighted_ref[...] * factor + fresh * intensity
        placed_ref[...] = placed_ref[...] * factor + fresh * depth_ref[g]

    @pl.when(step == pl.num_programs(0) - 1)
    def _():
        joined_ref[...] = weighted_ref[...] / total_ref[...]
        mean_ref[...] = placed_ref[...] / total_ref[...]


def propagate(taps, window, n_out):
    planes = taps.shape[0]
    _, n_in, width = window.shape
    block_count = width // LANE - 1
    stacked = window.reshape(2 * n_in, width)
    body = functools.partial(
        propagate_kernel, n_out=n_out, n_in=n_in, block_count=block_count
    )
    flops = 2 * planes * (2 * n_out * 2 * n_in * width + block_count * n_out * 4 * LANE * SPAN)
    return pl.pallas_call(
        body,
        grid=(1,),
        in_specs=[
            pl.BlockSpec((planes, 2, SPAN), lambda p: (0, 0, 0)),
            pl.BlockSpec((2 * n_in, width), lambda p: (0, 0)),
        ],
        out_specs=pl.BlockSpec((planes, n_out, block_count * LANE), lambda p: (0, 0, 0)),
        out_shape=jax.ShapeDtypeStruct((planes, n_out, block_count * LANE), jnp.float32),
        cost_estimate=pl.CostEstimate(
            flops=flops,
            transcendentals=0,
            bytes_accessed=stacked.size * 2 + planes * n_out * block_count * LANE * 4,
        ),
    )(taps, stacked)


def joining(corner, taps, prior, depth_values, window, n_out, bounds):
    planes = taps.shape[0]
    group = 8 if planes % 8 == 0 else planes
    _, n_in, width = window.shape
    block_count = width // LANE - 1
    stacked = window.reshape(2 * n_in, width)
    body = functools.partial(
        joining_kernel, n_out=n_out, n_in=n_in, block_count=block_count, bounds=bounds
    )
    out_cols = block_count * LANE
    flops = 2 * planes * (2 * n_out * 2 * n_in * width + block_count * n_out * 4 * LANE * SPAN)
    grid_spec = pltpu.PrefetchScalarGridSpec(
        num_scalar_prefetch=1,
        grid=(planes // group,),
        in_specs=[
            pl.BlockSpec((group, 2, SPAN), lambda p, c: (p, 0, 0)),
            pl.BlockSpec((group, n_out, 1), lambda p, c: (p, 0, 0)),
            pl.BlockSpec((group, 1, 1), lambda p, c: (p, 0, 0)),
            pl.BlockSpec((2 * n_in, width), lambda p, c: (0, 0)),
        ],
        out_specs=[
            pl.BlockSpec((n_out, out_cols), lambda p, c: (0, 0)),
            pl.BlockSpec((n_out, out_cols), lambda p, c: (0, 0)),
        ],
        scratch_shapes=[pltpu.VMEM((n_out, out_cols), jnp.float32) for _ in range(4)],
    )
    return pl.pallas_call(
        body,
        grid_spec=grid_spec,
        out_shape=[jax.ShapeDtypeStruct((n_out, out_cols), jnp.float32)] * 2,
        compiler_params=pltpu.CompilerParams(dimension_semantics=("arbitrary",)),
        cost_estimate=pl.CostEstimate(
            flops=flops,
            transcendentals=3 * planes * n_out * out_cols,
            bytes_accessed=stacked.size * 2 + 2 * n_out * out_cols * 4,
        ),
    )(corner, taps, prior, depth_values, stacked)


def gather_depth(block):
    count = lax.axis_size("depth")
    moved = [
        lax.ppermute(block, "depth", [((j + shift) % count, j) for j in range(count)])
        for shift in range(1, count)
    ]
    return jnp.concatenate([block, *moved], axis=0)


def local(hologram, kernel, depth_prior):
    _, rows, col_total = hologram.shape
    local_planes = kernel.shape[0]
    depth_count = lax.axis_size("depth")
    tile_count = lax.axis_size("tile")
    depth_at = lax.axis_index("depth")
    tile_at = lax.axis_index("tile")
    planes_total = local_planes * depth_count
    own_cols = col_total // depth_count
    row_total = rows * tile_count
    half_taps = TAPS // 2

    taps = jnp.pad(kernel.astype(jnp.float32), ((0, 0), (0, 0), (0, SPAN - TAPS)))
    packed = jnp.concatenate([taps.reshape(local_planes, 2 * SPAN), depth_prior], axis=1)
    packed_all = gather_depth(packed)
    owner = (depth_at + jnp.arange(planes_total) // local_planes) % depth_count
    plane_at = owner * local_planes + jnp.arange(planes_total) % local_planes

    halo = 48
    above = lax.ppermute(
        hologram[:, rows - halo :], "tile", [(i, i + 1) for i in range(tile_count - 1)]
    )
    below = lax.ppermute(hologram[:, :halo], "tile", [(i + 1, i) for i in range(tile_count - 1)])
    extended = jnp.concatenate([above, hologram, below], axis=1)

    window = extended[:, halo - half_taps : halo - half_taps + LANE]
    window = jnp.pad(window, ((0, 0), (0, 0), (half_taps, LANE - half_taps)))
    plane_stack = propagate(taps, window, rows)
    plane_stack, packed_all = lax.optimization_barrier((plane_stack, packed_all))
    taps_all = packed_all[:, : 2 * SPAN].reshape(planes_total, 2, SPAN)
    prior_all = packed_all[:, 2 * SPAN :]

    lead_rows = 8
    n_out = rows + 2 * lead_rows
    first = halo - half_taps - lead_rows
    window = extended[:, first : first + n_out + TAPS - 1]
    lead = LANE // 2 + half_taps
    width = own_cols + 2 * LANE
    window = jnp.pad(
        window, ((0, 0), (0, SPAN - window.shape[1]), (lead, width - lead))
    )
    window = lax.dynamic_slice_in_dim(window, depth_at * own_cols, width, axis=2)
    corner = jnp.stack([tile_at * rows - lead_rows, depth_at * own_cols - LANE // 2]).astype(
        jnp.int32
    )
    prior_rows = jnp.pad(prior_all, ((0, 0), (lead_rows, lead_rows)))[:, :, None]
    depth_values = ((plane_at.astype(jnp.float32) + 0.5) / planes_total)[:, None, None]
    joined, mean_depth = joining(
        corner, taps_all, prior_rows, depth_values, window, n_out, (row_total, col_total)
    )
    start = LANE // 2
    joined = joined[lead_rows : lead_rows + rows, start : start + own_cols]
    mean_depth = mean_depth[lead_rows : lead_rows + rows, start : start + own_cols]
    return (plane_stack, joined, mean_depth)


def solution(mesh):
    in_specs = (P(None, "tile", None), P("depth", None, None), P("depth", "tile"))
    out_specs = (P("depth", "tile", None), P("tile", "depth"), P("tile", "depth"))
    return jax.shard_map(local, mesh=mesh, in_specs=in_specs, out_specs=out_specs, check_vma=False)
```

```python
import functools

import jax
import jax.numpy as jnp
from jax import lax
from jax.experimental import pallas as pl
from jax.experimental.pallas import tpu as pltpu
from jax.sharding import PartitionSpec as P

TAPS = 64
LANE = 128
SPAN = 2 * LANE


def skews(taps_ref, plane):
    def skew(taps):
        return pltpu.roll(jnp.broadcast_to(taps, (LANE, SPAN)), 0, 1, stride=1, stride_axis=0)

    return skew(taps_ref[plane, 0:1, :]), skew(taps_ref[plane, 1:2, :])


def rows_matrix(skew_re, skew_im, n_out, n_in):
    rows_re = skew_re[:n_out, :n_in]
    rows_im = skew_im[:n_out, :n_in]
    return jnp.concatenate(
        [
            jnp.concatenate([rows_re, -rows_im], axis=1),
            jnp.concatenate([rows_im, rows_re], axis=1),
        ],
        axis=0,
    ).astype(jnp.bfloat16)


def across_planes(taps_ref, window_ref, n_out, n_in):
    group = taps_ref.shape[0]
    skewed = [skews(taps_ref, g) for g in range(group)]
    matrix = jnp.concatenate([rows_matrix(*sk, n_out, n_in) for sk in skewed], axis=0)
    across = jnp.dot(matrix, window_ref[...], preferred_element_type=jnp.float32)
    return skewed, across.astype(jnp.bfloat16)


def column_intensity(across, skew_re, skew_im, n_out, block_count):
    across_re = across[:n_out]
    across_im = across[n_out:]

    def stacked(signal, first):
        return jnp.concatenate(
            [signal[:, LANE * b : LANE * (b + 1)] for b in range(first, first + block_count)], axis=0
        )

    blocks = jnp.concatenate(
        [stacked(across_re, 0), stacked(across_re, 1), stacked(across_im, 0), stacked(across_im, 1)],
        axis=1,
    )
    near_re = skew_re[:, :LANE].T
    far_re = skew_re[:, LANE:].T
    near_im = skew_im[:, :LANE].T
    far_im = skew_im[:, LANE:].T
    cols_matrix = jnp.concatenate(
        [
            jnp.concatenate([near_re, near_im], axis=1),
            jnp.concatenate([far_re, far_im], axis=1),
            jnp.concatenate([-near_im, near_re], axis=1),
            jnp.concatenate([-far_im, far_re], axis=1),
        ],
        axis=0,
    ).astype(jnp.bfloat16)
    field = jnp.dot(blocks, cols_matrix, preferred_element_type=jnp.float32)
    return field[:, :LANE] * field[:, :LANE] + field[:, LANE:] * field[:, LANE:]


def propagate_kernel(taps_ref, window_ref, out_ref, *, n_out, n_in, block_count):
    skewed, across = across_planes(taps_ref, window_ref, n_out, n_in)
    for g, (skew_re, skew_im) in enumerate(skewed):
        intensity = column_intensity(
            across[2 * n_out * g : 2 * n_out * (g + 1)], skew_re, skew_im, n_out, block_count
        )
        for b in range(block_count):
            out_ref[g, :, LANE * b : LANE * (b + 1)] = intensity[n_out * b : n_out * (b + 1)]


def joining_kernel(
    corner_ref, taps_ref, prior_ref, depth_ref, window_ref, joined_ref, mean_ref,
    total_ref, weighted_ref, placed_ref, *, n_out, n_in, block_count, bounds, crop,
):
    step = pl.program_id(0)

    @pl.when(step == 0)
    def _():
        total_ref[...] = jnp.zeros(total_ref.shape, jnp.float32)
        weighted_ref[...] = jnp.zeros(weighted_ref.shape, jnp.float32)
        placed_ref[...] = jnp.zeros(placed_ref.shape, jnp.float32)

    skewed, across = across_planes(taps_ref, window_ref, n_out, n_in)
    height, width = n_out, block_count * LANE
    row_at = corner_ref[0] + lax.broadcasted_iota(jnp.int32, (height, width), 0)
    col_at = corner_ref[1] + lax.broadcasted_iota(jnp.int32, (height, width), 1)
    inside = (row_at >= 0) & (row_at < bounds[0]) & (col_at >= 0) & (col_at < bounds[1])
    for g, (skew_re, skew_im) in enumerate(skewed):
        stacked = column_intensity(
            across[2 * n_out * g : 2 * n_out * (g + 1)], skew_re, skew_im, n_out, block_count
        )
        intensity = jnp.concatenate(
            [stacked[n_out * b : n_out * (b + 1)] for b in range(block_count)], axis=1
        )
        intensity = jnp.where(inside, intensity, 0.0)
        vertical = (
            pltpu.roll(intensity, 1, 0) + 2.0 * intensity + pltpu.roll(intensity, height - 1, 0)
        )
        grad_x = pltpu.roll(vertical, width - 1, 1) - pltpu.roll(vertical, 1, 1)
        horizontal = (
            pltpu.roll(intensity, 1, 1) + 2.0 * intensity + pltpu.roll(intensity, width - 1, 1)
        )
        grad_y = pltpu.roll(horizontal, height - 1, 0) - pltpu.roll(horizontal, 1, 0)
        fresh = prior_ref[g] * (1.0 + (grad_x * grad_x + grad_y * grad_y))
        total_ref[...] = total_ref[...] + fresh
        weighted_ref[...] = weighted_ref[...] + fresh * intensity
        placed_ref[...] = placed_ref[...] + fresh * depth_ref[g]

    @pl.when(step == pl.num_programs(0) - 1)
    def _():
        rows, cols = joined_ref.shape
        top, left = crop

        def cropped(values):
            return pltpu.roll(values, width - left, 1)[top : top + rows, :cols]

        joined_ref[...] = cropped(weighted_ref[...] / total_ref[...])
        mean_ref[...] = cropped(placed_ref[...] / total_ref[...])


def propagate(taps, window, n_out):
    planes = taps.shape[0]
    _, n_in, width = window.shape
    block_count = width // LANE - 1
    stacked = window.reshape(2 * n_in, width)
    body = functools.partial(
        propagate_kernel, n_out=n_out, n_in=n_in, block_count=block_count
    )
    flops = 2 * planes * (2 * n_out * 2 * n_in * width + block_count * n_out * 4 * LANE * SPAN)
    return pl.pallas_call(
        body,
        grid=(1,),
        in_specs=[
            pl.BlockSpec((planes, 2, SPAN), lambda p: (0, 0, 0)),
            pl.BlockSpec((2 * n_in, width), lambda p: (0, 0)),
        ],
        out_specs=pl.BlockSpec((planes, n_out, block_count * LANE), lambda p: (0, 0, 0)),
        out_shape=jax.ShapeDtypeStruct((planes, n_out, block_count * LANE), jnp.float32),
        cost_estimate=pl.CostEstimate(
            flops=flops,
            transcendentals=0,
            bytes_accessed=stacked.size * 2 + planes * n_out * block_count * LANE * 4,
        ),
    )(taps, stacked)


def joining(corner, taps, prior, depth_values, window, n_out, bounds, crop, out_shape):
    planes = taps.shape[0]
    group = 8 if planes % 8 == 0 else planes
    _, n_in, width = window.shape
    block_count = width // LANE - 1
    stacked = window.reshape(2 * n_in, width)
    body = functools.partial(
        joining_kernel, n_out=n_out, n_in=n_in, block_count=block_count, bounds=bounds,
        crop=crop,
    )
    out_cols = block_count * LANE
    flops = 2 * planes * (2 * n_out * 2 * n_in * width + block_count * n_out * 4 * LANE * SPAN)
    grid_spec = pltpu.PrefetchScalarGridSpec(
        num_scalar_prefetch=1,
        grid=(planes // group,),
        in_specs=[
            pl.BlockSpec((group, 2, SPAN), lambda p, c: (p, 0, 0)),
            pl.BlockSpec((group, n_out, 1), lambda p, c: (p, 0, 0)),
            pl.BlockSpec((group, 1, 1), lambda p, c: (p, 0, 0)),
            pl.BlockSpec((2 * n_in, width), lambda p, c: (0, 0)),
        ],
        out_specs=[
            pl.BlockSpec(out_shape, lambda p, c: (0, 0)),
            pl.BlockSpec(out_shape, lambda p, c: (0, 0)),
        ],
        scratch_shapes=[pltpu.VMEM((n_out, out_cols), jnp.float32) for _ in range(3)],
    )
    return pl.pallas_call(
        body,
        grid_spec=grid_spec,
        out_shape=[jax.ShapeDtypeStruct(out_shape, jnp.float32)] * 2,
        compiler_params=pltpu.CompilerParams(dimension_semantics=("arbitrary",)),
        cost_estimate=pl.CostEstimate(
            flops=flops,
            transcendentals=0,
            bytes_accessed=stacked.size * 2 + 2 * n_out * out_cols * 4,
        ),
    )(corner, taps, prior, depth_values, stacked)


def gather_depth(block):
    count = lax.axis_size("depth")
    placed = jnp.zeros((count * block.shape[0], block.shape[1]), block.dtype)
    placed = lax.dynamic_update_slice_in_dim(
        placed, block, lax.axis_index("depth") * block.shape[0], axis=0
    )
    return lax.psum(placed, "depth")


def local(hologram, kernel, depth_prior):
    _, rows, col_total = hologram.shape
    local_planes = kernel.shape[0]
    depth_count = lax.axis_size("depth")
    tile_count = lax.axis_size("tile")
    depth_at = lax.axis_index("depth")
    tile_at = lax.axis_index("tile")
    planes_total = local_planes * depth_count
    own_cols = col_total // depth_count
    row_total = rows * tile_count
    half_taps = TAPS // 2

    taps = jnp.pad(kernel.astype(jnp.float32), ((0, 0), (0, 0), (0, SPAN - TAPS)))
    packed = jnp.concatenate([taps.reshape(local_planes, 2 * SPAN), depth_prior], axis=1)
    packed_all = gather_depth(packed)
    plane_at = jnp.arange(planes_total)

    halo = 48
    above = lax.ppermute(
        hologram[:, rows - halo :], "tile", [(i, i + 1) for i in range(tile_count - 1)]
    )
    below = lax.ppermute(hologram[:, :halo], "tile", [(i + 1, i) for i in range(tile_count - 1)])
    extended = jnp.concatenate([above, hologram, below], axis=1)

    window = extended[:, halo - half_taps : halo - half_taps + LANE]
    window = jnp.pad(window, ((0, 0), (0, 0), (half_taps, LANE - half_taps)))
    plane_stack = propagate(taps, window, rows)
    plane_stack, packed_all = lax.optimization_barrier((plane_stack, packed_all))
    taps_all = packed_all[:, : 2 * SPAN].reshape(planes_total, 2, SPAN)
    prior_all = packed_all[:, 2 * SPAN :]

    lead_rows = 8
    n_out = rows + 2 * lead_rows
    first = halo - half_taps - lead_rows
    window = extended[:, first : first + n_out + TAPS - 1]
    lead = LANE // 2 + half_taps
    width = own_cols + 2 * LANE
    window = jnp.pad(
        window, ((0, 0), (0, SPAN - window.shape[1]), (lead, width - lead))
    )
    window = lax.dynamic_slice_in_dim(window, depth_at * own_cols, width, axis=2)
    corner = jnp.stack([tile_at * rows - lead_rows, depth_at * own_cols - LANE // 2]).astype(
        jnp.int32
    )
    prior_weight = jnp.exp(prior_all - jnp.max(prior_all, axis=0, keepdims=True))
    prior_rows = jnp.pad(prior_weight, ((0, 0), (lead_rows, lead_rows)), constant_values=1.0)
    depth_values = ((plane_at.astype(jnp.float32) + 0.5) / planes_total)[:, None, None]
    joined, mean_depth = joining(
        corner, taps_all, prior_rows[:, :, None], depth_values, window, n_out,
        (row_total, col_total), (lead_rows, LANE // 2), (rows, own_cols),
    )
    return (plane_stack, joined, mean_depth)


def solution(mesh):
    in_specs = (P(None, "tile", None), P("depth", None, None), P("depth", "tile"))
    out_specs = (P("depth", "tile", None), P("tile", "depth"), P("tile", "depth"))
    return jax.shard_map(local, mesh=mesh, in_specs=in_specs, out_specs=out_specs, check_vma=False)
```

```python
import functools

import jax
import jax.numpy as jnp
from jax import lax
from jax.experimental import pallas as pl
from jax.experimental.pallas import tpu as pltpu
from jax.sharding import PartitionSpec as P

TAPS = 64
LANE = 128
SPAN = 2 * LANE


def skews(taps_ref, plane):
    def skew(taps):
        return pltpu.roll(jnp.broadcast_to(taps, (LANE, SPAN)), 0, 1, stride=1, stride_axis=0)

    return skew(taps_ref[plane, 0:1, :]), skew(taps_ref[plane, 1:2, :])


def rows_matrix(skew_re, skew_im, n_out, n_in):
    rows_re = skew_re[:n_out, :n_in]
    rows_im = skew_im[:n_out, :n_in]
    return jnp.concatenate(
        [
            jnp.concatenate([rows_re, -rows_im], axis=1),
            jnp.concatenate([rows_im, rows_re], axis=1),
        ],
        axis=0,
    ).astype(jnp.bfloat16)


def across_planes(taps_ref, window_ref, n_out, n_in):
    group = taps_ref.shape[0]
    skewed = [skews(taps_ref, g) for g in range(group)]
    matrix = jnp.concatenate([rows_matrix(*sk, n_out, n_in) for sk in skewed], axis=0)
    across = jnp.dot(matrix, window_ref[...], preferred_element_type=jnp.float32)
    return skewed, across.astype(jnp.bfloat16)


def column_intensity(across, skew_re, skew_im, n_out, block_count):
    across_re = across[:n_out]
    across_im = across[n_out:]

    def stacked(signal, first):
        return jnp.concatenate(
            [signal[:, LANE * b : LANE * (b + 1)] for b in range(first, first + block_count)], axis=0
        )

    blocks = jnp.concatenate(
        [stacked(across_re, 0), stacked(across_re, 1), stacked(across_im, 0), stacked(across_im, 1)],
        axis=1,
    )
    near_re = skew_re[:, :LANE].T
    far_re = skew_re[:, LANE:].T
    near_im = skew_im[:, :LANE].T
    far_im = skew_im[:, LANE:].T
    cols_matrix = jnp.concatenate(
        [
            jnp.concatenate([near_re, near_im], axis=1),
            jnp.concatenate([far_re, far_im], axis=1),
            jnp.concatenate([-near_im, near_re], axis=1),
            jnp.concatenate([-far_im, far_re], axis=1),
        ],
        axis=0,
    ).astype(jnp.bfloat16)
    field = jnp.dot(blocks, cols_matrix, preferred_element_type=jnp.float32)
    return field[:, :LANE] * field[:, :LANE] + field[:, LANE:] * field[:, LANE:]


def propagate_kernel(taps_ref, window_ref, out_ref, *, n_out, n_in, block_count):
    skewed, across = across_planes(taps_ref, window_ref, n_out, n_in)
    for g, (skew_re, skew_im) in enumerate(skewed):
        intensity = column_intensity(
            across[2 * n_out * g : 2 * n_out * (g + 1)], skew_re, skew_im, n_out, block_count
        )
        for b in range(block_count):
            out_ref[g, :, LANE * b : LANE * (b + 1)] = intensity[n_out * b : n_out * (b + 1)]


def joining_kernel(
    corner_ref, taps_ref, prior_ref, depth_ref, window_ref, joined_ref, mean_ref,
    total_ref, weighted_ref, placed_ref, *, n_out, n_in, block_count, bounds, crop,
):
    step = pl.program_id(0)

    @pl.when(step == 0)
    def _():
        total_ref[...] = jnp.zeros(total_ref.shape, jnp.float32)
        weighted_ref[...] = jnp.zeros(weighted_ref.shape, jnp.float32)
        placed_ref[...] = jnp.zeros(placed_ref.shape, jnp.float32)

    skewed, across = across_planes(taps_ref, window_ref, n_out, n_in)
    height, width = n_out, block_count * LANE
    row_at = corner_ref[0] + lax.broadcasted_iota(jnp.int32, (height, width), 0)
    col_at = corner_ref[1] + lax.broadcasted_iota(jnp.int32, (height, width), 1)
    inside = (row_at >= 0) & (row_at < bounds[0]) & (col_at >= 0) & (col_at < bounds[1])
    for g, (skew_re, skew_im) in enumerate(skewed):
        stacked = column_intensity(
            across[2 * n_out * g : 2 * n_out * (g + 1)], skew_re, skew_im, n_out, block_count
        )
        intensity = jnp.concatenate(
            [stacked[n_out * b : n_out * (b + 1)] for b in range(block_count)], axis=1
        )
        intensity = jnp.where(inside, intensity, 0.0)
        vertical = (
            pltpu.roll(intensity, 1, 0) + 2.0 * intensity + pltpu.roll(intensity, height - 1, 0)
        )
        grad_x = pltpu.roll(vertical, width - 1, 1) - pltpu.roll(vertical, 1, 1)
        horizontal = (
            pltpu.roll(intensity, 1, 1) + 2.0 * intensity + pltpu.roll(intensity, width - 1, 1)
        )
        grad_y = pltpu.roll(horizontal, height - 1, 0) - pltpu.roll(horizontal, 1, 0)
        fresh = prior_ref[g] * (1.0 + (grad_x * grad_x + grad_y * grad_y))
        total_ref[...] = total_ref[...] + fresh
        weighted_ref[...] = weighted_ref[...] + fresh * intensity
        placed_ref[...] = placed_ref[...] + fresh * depth_ref[g]

    @pl.when(step == pl.num_programs(0) - 1)
    def _():
        rows, cols = joined_ref.shape
        top, left = crop

        def cropped(values):
            return pltpu.roll(values, width - left, 1)[top : top + rows, :cols]

        joined_ref[...] = cropped(weighted_ref[...] / total_ref[...])
        mean_ref[...] = cropped(placed_ref[...] / total_ref[...])


def propagate(taps, window, n_out):
    planes = taps.shape[0]
    _, n_in, width = window.shape
    block_count = width // LANE - 1
    stacked = window.reshape(2 * n_in, width)
    body = functools.partial(
        propagate_kernel, n_out=n_out, n_in=n_in, block_count=block_count
    )
    flops = 2 * planes * (2 * n_out * 2 * n_in * width + block_count * n_out * 4 * LANE * SPAN)
    return pl.pallas_call(
        body,
        grid=(1,),
        in_specs=[
            pl.BlockSpec((planes, 2, SPAN), lambda p: (0, 0, 0)),
            pl.BlockSpec((2 * n_in, width), lambda p: (0, 0)),
        ],
        out_specs=pl.BlockSpec((planes, n_out, block_count * LANE), lambda p: (0, 0, 0)),
        out_shape=jax.ShapeDtypeStruct((planes, n_out, block_count * LANE), jnp.float32),
        cost_estimate=pl.CostEstimate(
            flops=flops,
            transcendentals=0,
            bytes_accessed=stacked.size * 2 + planes * n_out * block_count * LANE * 4,
        ),
    )(taps, stacked)


def joining(corner, taps, prior, depth_values, window, n_out, bounds, crop, out_shape):
    planes = taps.shape[0]
    group = 8 if planes % 8 == 0 else planes
    _, n_in, width = window.shape
    block_count = width // LANE - 1
    stacked = window.reshape(2 * n_in, width)
    body = functools.partial(
        joining_kernel, n_out=n_out, n_in=n_in, block_count=block_count, bounds=bounds,
        crop=crop,
    )
    out_cols = block_count * LANE
    flops = 2 * planes * (2 * n_out * 2 * n_in * width + block_count * n_out * 4 * LANE * SPAN)
    grid_spec = pltpu.PrefetchScalarGridSpec(
        num_scalar_prefetch=1,
        grid=(planes // group,),
        in_specs=[
            pl.BlockSpec((group, 2, SPAN), lambda p, c: (p, 0, 0)),
            pl.BlockSpec((group, n_out, 1), lambda p, c: (p, 0, 0)),
            pl.BlockSpec((group, 1, 1), lambda p, c: (p, 0, 0)),
            pl.BlockSpec((2 * n_in, width), lambda p, c: (0, 0)),
        ],
        out_specs=[
            pl.BlockSpec(out_shape, lambda p, c: (0, 0)),
            pl.BlockSpec(out_shape, lambda p, c: (0, 0)),
        ],
        scratch_shapes=[pltpu.VMEM((n_out, out_cols), jnp.float32) for _ in range(3)],
    )
    return pl.pallas_call(
        body,
        grid_spec=grid_spec,
        out_shape=[jax.ShapeDtypeStruct(out_shape, jnp.float32)] * 2,
        compiler_params=pltpu.CompilerParams(dimension_semantics=("arbitrary",)),
        cost_estimate=pl.CostEstimate(
            flops=flops,
            transcendentals=0,
            bytes_accessed=stacked.size * 2 + 2 * n_out * out_cols * 4,
        ),
    )(corner, taps, prior, depth_values, stacked)


def gather_depth(block):
    count = lax.axis_size("depth")
    moved = [
        lax.ppermute(block, "depth", [((j + shift) % count, j) for j in range(count)])
        for shift in range(1, count)
    ]
    return jnp.concatenate([block, *moved], axis=0)


def local(hologram, kernel, depth_prior):
    _, rows, col_total = hologram.shape
    local_planes = kernel.shape[0]
    depth_count = lax.axis_size("depth")
    tile_count = lax.axis_size("tile")
    depth_at = lax.axis_index("depth")
    tile_at = lax.axis_index("tile")
    planes_total = local_planes * depth_count
    own_cols = col_total // depth_count
    row_total = rows * tile_count
    half_taps = TAPS // 2

    taps = jnp.pad(kernel.astype(jnp.float32), ((0, 0), (0, 0), (0, SPAN - TAPS)))
    packed = jnp.concatenate([taps.reshape(local_planes, 2 * SPAN), depth_prior], axis=1)
    packed_all = gather_depth(packed)
    owner = (depth_at + jnp.arange(planes_total) // local_planes) % depth_count
    plane_at = owner * local_planes + jnp.arange(planes_total) % local_planes

    halo = 48
    above = lax.ppermute(
        hologram[:, rows - halo :], "tile", [(i, i + 1) for i in range(tile_count - 1)]
    )
    below = lax.ppermute(hologram[:, :halo], "tile", [(i + 1, i) for i in range(tile_count - 1)])
    extended = jnp.concatenate([above, hologram, below], axis=1)

    window = extended[:, halo - half_taps : halo - half_taps + LANE]
    window = jnp.pad(window, ((0, 0), (0, 0), (half_taps, LANE - half_taps)))
    plane_stack = propagate(taps, window, rows)
    plane_stack, packed_all = lax.optimization_barrier((plane_stack, packed_all))
    taps_all = packed_all[:, : 2 * SPAN].reshape(planes_total, 2, SPAN)
    prior_all = packed_all[:, 2 * SPAN :]

    lead_rows = 8
    n_out = rows + 2 * lead_rows
    first = halo - half_taps - lead_rows
    window = extended[:, first : first + n_out + TAPS - 1]
    lead = LANE // 2 + half_taps
    width = own_cols + 2 * LANE
    window = jnp.pad(
        window, ((0, 0), (0, SPAN - window.shape[1]), (lead, width - lead))
    )
    window = lax.dynamic_slice_in_dim(window, depth_at * own_cols, width, axis=2)
    corner = jnp.stack([tile_at * rows - lead_rows, depth_at * own_cols - LANE // 2]).astype(
        jnp.int32
    )
    prior_weight = jnp.exp(prior_all - jnp.max(prior_all, axis=0, keepdims=True))
    prior_rows = jnp.pad(prior_weight, ((0, 0), (lead_rows, lead_rows)), constant_values=1.0)
    depth_values = ((plane_at.astype(jnp.float32) + 0.5) / planes_total)[:, None, None]
    joined, mean_depth = joining(
        corner, taps_all, prior_rows[:, :, None], depth_values, window, n_out,
        (row_total, col_total), (lead_rows, LANE // 2), (rows, own_cols),
    )
    return (plane_stack, joined, mean_depth)


def solution(mesh):
    in_specs = (P(None, "tile", None), P("depth", None, None), P("depth", "tile"))
    out_specs = (P("depth", "tile", None), P("tile", "depth"), P("tile", "depth"))
    return jax.shard_map(local, mesh=mesh, in_specs=in_specs, out_specs=out_specs, check_vma=False)
```

```python
import functools

import jax
import jax.numpy as jnp
from jax import lax
from jax.experimental import pallas as pl
from jax.experimental.pallas import tpu as pltpu
from jax.sharding import PartitionSpec as P

TAPS = 64
LANE = 128
SPAN = 2 * LANE


def skews(taps_ref, plane):
    def skew(taps):
        return pltpu.roll(jnp.broadcast_to(taps, (LANE, SPAN)), 0, 1, stride=1, stride_axis=0)

    return skew(taps_ref[plane, 0:1, :]), skew(taps_ref[plane, 1:2, :])


def rows_matrix(skew_re, skew_im, n_out, n_in):
    rows_re = skew_re[:n_out, :n_in]
    rows_im = skew_im[:n_out, :n_in]
    return jnp.concatenate(
        [
            jnp.concatenate([rows_re, -rows_im], axis=1),
            jnp.concatenate([rows_im, rows_re], axis=1),
        ],
        axis=0,
    ).astype(jnp.bfloat16)


def across_planes(taps_ref, window_ref, n_out, n_in, starts):
    group = taps_ref.shape[0]
    skewed = [skews(taps_ref, g) for g in range(group)]
    matrix = jnp.concatenate([rows_matrix(*sk, n_out, n_in) for sk in skewed], axis=0)
    across = jnp.dot(
        matrix[:, :n_in], window_ref[starts[0] : starts[0] + n_in], preferred_element_type=jnp.float32
    ) + jnp.dot(
        matrix[:, n_in:], window_ref[starts[1] : starts[1] + n_in], preferred_element_type=jnp.float32
    )
    return skewed, across.astype(jnp.bfloat16)


def column_intensity(across, skew_re, skew_im, n_out, block_count):
    across_re = across[:n_out]
    across_im = across[n_out:]

    def stacked(signal, first):
        return jnp.concatenate(
            [signal[:, LANE * b : LANE * (b + 1)] for b in range(first, first + block_count)], axis=0
        )

    blocks = jnp.concatenate(
        [stacked(across_re, 0), stacked(across_re, 1), stacked(across_im, 0), stacked(across_im, 1)],
        axis=1,
    )
    near_re = skew_re[:, :LANE].T
    far_re = skew_re[:, LANE:].T
    near_im = skew_im[:, :LANE].T
    far_im = skew_im[:, LANE:].T
    cols_matrix = jnp.concatenate(
        [
            jnp.concatenate([near_re, near_im], axis=1),
            jnp.concatenate([far_re, far_im], axis=1),
            jnp.concatenate([-near_im, near_re], axis=1),
            jnp.concatenate([-far_im, far_re], axis=1),
        ],
        axis=0,
    ).astype(jnp.bfloat16)
    field = jnp.dot(blocks, cols_matrix, preferred_element_type=jnp.float32)
    return field[:, :LANE] * field[:, :LANE] + field[:, LANE:] * field[:, LANE:]


def propagate_kernel(taps_ref, window_ref, out_ref, *, n_out, n_in, block_count, starts):
    skewed, across = across_planes(taps_ref, window_ref, n_out, n_in, starts)
    for g, (skew_re, skew_im) in enumerate(skewed):
        intensity = column_intensity(
            across[2 * n_out * g : 2 * n_out * (g + 1)], skew_re, skew_im, n_out, block_count
        )
        for b in range(block_count):
            out_ref[g, :, LANE * b : LANE * (b + 1)] = intensity[n_out * b : n_out * (b + 1)]


def joining_kernel(
    corner_ref, taps_ref, prior_ref, depth_ref, window_ref, joined_ref, mean_ref,
    total_ref, weighted_ref, placed_ref, *, n_out, n_in, block_count, bounds, crop,
):
    step = pl.program_id(0)

    @pl.when(step == 0)
    def _():
        total_ref[...] = jnp.zeros(total_ref.shape, jnp.float32)
        weighted_ref[...] = jnp.zeros(weighted_ref.shape, jnp.float32)
        placed_ref[...] = jnp.zeros(placed_ref.shape, jnp.float32)

    skewed, across = across_planes(taps_ref, window_ref, n_out, n_in, (0, n_in))
    height, width = n_out, block_count * LANE
    row_at = corner_ref[0] + lax.broadcasted_iota(jnp.int32, (height, width), 0)
    col_at = corner_ref[1] + lax.broadcasted_iota(jnp.int32, (height, width), 1)
    inside = (row_at >= 0) & (row_at < bounds[0]) & (col_at >= 0) & (col_at < bounds[1])
    for g, (skew_re, skew_im) in enumerate(skewed):
        stacked = column_intensity(
            across[2 * n_out * g : 2 * n_out * (g + 1)], skew_re, skew_im, n_out, block_count
        )
        intensity = jnp.concatenate(
            [stacked[n_out * b : n_out * (b + 1)] for b in range(block_count)], axis=1
        )
        intensity = jnp.where(inside, intensity, 0.0)
        vertical = (
            pltpu.roll(intensity, 1, 0) + 2.0 * intensity + pltpu.roll(intensity, height - 1, 0)
        )
        grad_x = pltpu.roll(vertical, width - 1, 1) - pltpu.roll(vertical, 1, 1)
        horizontal = (
            pltpu.roll(intensity, 1, 1) + 2.0 * intensity + pltpu.roll(intensity, width - 1, 1)
        )
        grad_y = pltpu.roll(horizontal, height - 1, 0) - pltpu.roll(horizontal, 1, 0)
        fresh = prior_ref[g] * (1.0 + (grad_x * grad_x + grad_y * grad_y))
        total_ref[...] = total_ref[...] + fresh
        weighted_ref[...] = weighted_ref[...] + fresh * intensity
        placed_ref[...] = placed_ref[...] + fresh * depth_ref[g]

    @pl.when(step == pl.num_programs(0) - 1)
    def _():
        rows, cols = joined_ref.shape
        top, left = crop

        def cropped(values):
            return pltpu.roll(values, width - left, 1)[top : top + rows, :cols]

        joined_ref[...] = cropped(weighted_ref[...] / total_ref[...])
        mean_ref[...] = cropped(placed_ref[...] / total_ref[...])


def propagate(taps, window, n_out, first_row):
    planes = taps.shape[0]
    _, window_rows, width = window.shape
    n_in = n_out + TAPS
    block_count = width // LANE - 1
    stacked = window.reshape(2 * window_rows, width)
    body = functools.partial(
        propagate_kernel, n_out=n_out, n_in=n_in, block_count=block_count,
        starts=(first_row, window_rows + first_row),
    )
    flops = 2 * planes * (2 * n_out * 2 * n_in * width + block_count * n_out * 4 * LANE * SPAN)
    return pl.pallas_call(
        body,
        grid=(1,),
        in_specs=[
            pl.BlockSpec((planes, 2, SPAN), lambda p: (0, 0, 0)),
            pl.BlockSpec((2 * window_rows, width), lambda p: (0, 0)),
        ],
        out_specs=pl.BlockSpec((planes, n_out, block_count * LANE), lambda p: (0, 0, 0)),
        out_shape=jax.ShapeDtypeStruct((planes, n_out, block_count * LANE), jnp.float32),
        cost_estimate=pl.CostEstimate(
            flops=flops,
            transcendentals=0,
            bytes_accessed=stacked.size * 2 + planes * n_out * block_count * LANE * 4,
        ),
    )(taps, stacked)


def joining(corner, taps, prior, depth_values, window, n_out, bounds, crop, out_shape):
    planes = taps.shape[0]
    group = 8 if planes % 8 == 0 else planes
    _, n_in, width = window.shape
    block_count = width // LANE - 1
    stacked = window.reshape(2 * n_in, width)
    body = functools.partial(
        joining_kernel, n_out=n_out, n_in=n_in, block_count=block_count, bounds=bounds,
        crop=crop,
    )
    out_cols = block_count * LANE
    flops = 2 * planes * (2 * n_out * 2 * n_in * width + block_count * n_out * 4 * LANE * SPAN)
    grid_spec = pltpu.PrefetchScalarGridSpec(
        num_scalar_prefetch=1,
        grid=(planes // group,),
        in_specs=[
            pl.BlockSpec((group, 2, SPAN), lambda p, c: (p, 0, 0)),
            pl.BlockSpec((group, n_out, 1), lambda p, c: (p, 0, 0)),
            pl.BlockSpec((group, 1, 1), lambda p, c: (p, 0, 0)),
            pl.BlockSpec((2 * n_in, width), lambda p, c: (0, 0)),
        ],
        out_specs=[
            pl.BlockSpec(out_shape, lambda p, c: (0, 0)),
            pl.BlockSpec(out_shape, lambda p, c: (0, 0)),
        ],
        scratch_shapes=[pltpu.VMEM((n_out, out_cols), jnp.float32) for _ in range(3)],
    )
    return pl.pallas_call(
        body,
        grid_spec=grid_spec,
        out_shape=[jax.ShapeDtypeStruct(out_shape, jnp.float32)] * 2,
        compiler_params=pltpu.CompilerParams(dimension_semantics=("arbitrary",)),
        cost_estimate=pl.CostEstimate(
            flops=flops,
            transcendentals=0,
            bytes_accessed=stacked.size * 2 + 2 * n_out * out_cols * 4,
        ),
    )(corner, taps, prior, depth_values, stacked)


def gather_depth(block):
    count = lax.axis_size("depth")
    have = 1
    while have < count:
        moved = [
            lax.ppermute(block, "depth", [((j + have * m) % count, j) for j in range(count)])
            for m in range(1, 4)
            if have * m < count
        ]
        block = jnp.concatenate([block, *moved], axis=0)
        have *= 1 + len(moved)
    return block[: count * (block.shape[0] // have)]


def local(hologram, kernel, depth_prior):
    _, rows, col_total = hologram.shape
    local_planes = kernel.shape[0]
    depth_count = lax.axis_size("depth")
    tile_count = lax.axis_size("tile")
    depth_at = lax.axis_index("depth")
    tile_at = lax.axis_index("tile")
    planes_total = local_planes * depth_count
    own_cols = col_total // depth_count
    row_total = rows * tile_count
    half_taps = TAPS // 2

    taps = jnp.pad(kernel.astype(jnp.float32), ((0, 0), (0, 0), (0, SPAN - TAPS)))
    packed = jnp.concatenate([taps.reshape(local_planes, 2 * SPAN), depth_prior], axis=1)
    packed_all = gather_depth(packed)
    owner = (depth_at + jnp.arange(planes_total) // local_planes) % depth_count
    plane_at = owner * local_planes + jnp.arange(planes_total) % local_planes

    halo = 48
    padded = jnp.pad(hologram, ((0, 0), (0, 0), (half_taps, LANE - half_taps)))
    above = lax.ppermute(
        padded[:, rows - halo :], "tile", [(i, i + 1) for i in range(tile_count - 1)]
    )
    below = lax.ppermute(padded[:, :halo], "tile", [(i + 1, i) for i in range(tile_count - 1)])
    extended = jnp.concatenate([above, padded, below], axis=1)

    plane_stack = propagate(taps, extended, rows, halo - half_taps)
    plane_stack, packed_all = lax.optimization_barrier((plane_stack, packed_all))
    taps_all = packed_all[:, : 2 * SPAN].reshape(planes_total, 2, SPAN)
    prior_all = packed_all[:, 2 * SPAN :]

    lead_rows = 8
    n_out = rows + 2 * lead_rows
    first = halo - half_taps - lead_rows
    window = extended[:, first : first + n_out + TAPS - 1, half_taps : half_taps + col_total]
    lead = LANE // 2 + half_taps
    width = own_cols + 2 * LANE
    window = jnp.pad(
        window, ((0, 0), (0, SPAN - window.shape[1]), (lead, width - lead))
    )
    window = lax.dynamic_slice_in_dim(window, depth_at * own_cols, width, axis=2)
    corner = jnp.stack([tile_at * rows - lead_rows, depth_at * own_cols - LANE // 2]).astype(
        jnp.int32
    )
    prior_weight = jnp.exp(prior_all - jnp.max(prior_all, axis=0, keepdims=True))
    prior_rows = jnp.pad(prior_weight, ((0, 0), (lead_rows, lead_rows)), constant_values=1.0)
    depth_values = ((plane_at.astype(jnp.float32) + 0.5) / planes_total)[:, None, None]
    joined, mean_depth = joining(
        corner, taps_all, prior_rows[:, :, None], depth_values, window, n_out,
        (row_total, col_total), (lead_rows, LANE // 2), (rows, own_cols),
    )
    return (plane_stack, joined, mean_depth)


def solution(mesh):
    in_specs = (P(None, "tile", None), P("depth", None, None), P("depth", "tile"))
    out_specs = (P("depth", "tile", None), P("tile", "depth"), P("tile", "depth"))
    return jax.shard_map(local, mesh=mesh, in_specs=in_specs, out_specs=out_specs, check_vma=False)
```

```python
import functools

import jax
import jax.numpy as jnp
from jax import lax
from jax.experimental import pallas as pl
from jax.experimental.pallas import tpu as pltpu
from jax.sharding import PartitionSpec as P

TAPS = 64
LANE = 128
SPAN = 2 * LANE


def skews(taps_ref, plane):
    def skew(taps):
        return pltpu.roll(jnp.broadcast_to(taps, (LANE, SPAN)), 0, 1, stride=1, stride_axis=0)

    return skew(taps_ref[plane, 0:1, :]), skew(taps_ref[plane, 1:2, :])


def rows_matrix(skew_re, skew_im, n_out, n_in):
    rows_re = skew_re[:n_out, :n_in]
    rows_im = skew_im[:n_out, :n_in]
    return jnp.concatenate(
        [
            jnp.concatenate([rows_re, -rows_im], axis=1),
            jnp.concatenate([rows_im, rows_re], axis=1),
        ],
        axis=0,
    ).astype(jnp.bfloat16)


def across_planes(taps_ref, window_ref, n_out, n_in, starts):
    group = taps_ref.shape[0]
    skewed = [skews(taps_ref, g) for g in range(group)]
    matrix = jnp.concatenate([rows_matrix(*sk, n_out, n_in) for sk in skewed], axis=0)
    across = jnp.dot(
        matrix[:, :n_in], window_ref[starts[0] : starts[0] + n_in], preferred_element_type=jnp.float32
    ) + jnp.dot(
        matrix[:, n_in:], window_ref[starts[1] : starts[1] + n_in], preferred_element_type=jnp.float32
    )
    return skewed, across.astype(jnp.bfloat16)


def column_intensity(across, skew_re, skew_im, n_out, block_count):
    across_re = across[:n_out]
    across_im = across[n_out:]

    def stacked(signal, first):
        return jnp.concatenate(
            [signal[:, LANE * b : LANE * (b + 1)] for b in range(first, first + block_count)], axis=0
        )

    blocks = jnp.concatenate(
        [stacked(across_re, 0), stacked(across_re, 1), stacked(across_im, 0), stacked(across_im, 1)],
        axis=1,
    )
    near_re = skew_re[:, :LANE].T
    far_re = skew_re[:, LANE:].T
    near_im = skew_im[:, :LANE].T
    far_im = skew_im[:, LANE:].T
    cols_matrix = jnp.concatenate(
        [
            jnp.concatenate([near_re, near_im], axis=1),
            jnp.concatenate([far_re, far_im], axis=1),
            jnp.concatenate([-near_im, near_re], axis=1),
            jnp.concatenate([-far_im, far_re], axis=1),
        ],
        axis=0,
    ).astype(jnp.bfloat16)
    field = jnp.dot(blocks, cols_matrix, preferred_element_type=jnp.float32)
    return field[:, :LANE] * field[:, :LANE] + field[:, LANE:] * field[:, LANE:]


def propagate_kernel(taps_ref, window_ref, out_ref, *, n_out, n_in, block_count, starts):
    skewed, across = across_planes(taps_ref, window_ref, n_out, n_in, starts)
    for g, (skew_re, skew_im) in enumerate(skewed):
        intensity = column_intensity(
            across[2 * n_out * g : 2 * n_out * (g + 1)], skew_re, skew_im, n_out, block_count
        )
        for b in range(block_count):
            out_ref[g, :, LANE * b : LANE * (b + 1)] = intensity[n_out * b : n_out * (b + 1)]


def joining_kernel(
    corner_ref, taps_ref, prior_ref, depth_ref, window_ref, joined_ref, mean_ref,
    total_ref, weighted_ref, placed_ref, *, n_out, n_in, block_count, bounds, crop,
):
    step = pl.program_id(0)

    @pl.when(step == 0)
    def _():
        total_ref[...] = jnp.zeros(total_ref.shape, jnp.float32)
        weighted_ref[...] = jnp.zeros(weighted_ref.shape, jnp.float32)
        placed_ref[...] = jnp.zeros(placed_ref.shape, jnp.float32)

    skewed, across = across_planes(taps_ref, window_ref, n_out, n_in, (0, n_in))
    height, width = n_out, block_count * LANE
    row_at = corner_ref[0] + lax.broadcasted_iota(jnp.int32, (height, width), 0)
    col_at = corner_ref[1] + lax.broadcasted_iota(jnp.int32, (height, width), 1)
    inside = (row_at >= 0) & (row_at < bounds[0]) & (col_at >= 0) & (col_at < bounds[1])
    for g, (skew_re, skew_im) in enumerate(skewed):
        stacked = column_intensity(
            across[2 * n_out * g : 2 * n_out * (g + 1)], skew_re, skew_im, n_out, block_count
        )
        intensity = jnp.concatenate(
            [stacked[n_out * b : n_out * (b + 1)] for b in range(block_count)], axis=1
        )
        intensity = jnp.where(inside, intensity, 0.0)
        vertical = (
            pltpu.roll(intensity, 1, 0) + 2.0 * intensity + pltpu.roll(intensity, height - 1, 0)
        )
        grad_x = pltpu.roll(vertical, width - 1, 1) - pltpu.roll(vertical, 1, 1)
        horizontal = (
            pltpu.roll(intensity, 1, 1) + 2.0 * intensity + pltpu.roll(intensity, width - 1, 1)
        )
        grad_y = pltpu.roll(horizontal, height - 1, 0) - pltpu.roll(horizontal, 1, 0)
        fresh = prior_ref[g] * (1.0 + (grad_x * grad_x + grad_y * grad_y))
        total_ref[...] = total_ref[...] + fresh
        weighted_ref[...] = weighted_ref[...] + fresh * intensity
        placed_ref[...] = placed_ref[...] + fresh * depth_ref[g]

    @pl.when(step == pl.num_programs(0) - 1)
    def _():
        rows, cols = joined_ref.shape
        top, left = crop

        def cropped(values):
            return pltpu.roll(values, width - left, 1)[top : top + rows, :cols]

        joined_ref[...] = cropped(weighted_ref[...] / total_ref[...])
        mean_ref[...] = cropped(placed_ref[...] / total_ref[...])


def propagate(taps, window, n_out, first_row):
    planes = taps.shape[0]
    _, window_rows, width = window.shape
    n_in = n_out + TAPS
    block_count = width // LANE - 1
    stacked = window.reshape(2 * window_rows, width)
    body = functools.partial(
        propagate_kernel, n_out=n_out, n_in=n_in, block_count=block_count,
        starts=(first_row, window_rows + first_row),
    )
    flops = 2 * planes * (2 * n_out * 2 * n_in * width + block_count * n_out * 4 * LANE * SPAN)
    return pl.pallas_call(
        body,
        grid=(planes,),
        in_specs=[
            pl.BlockSpec((1, 2, SPAN), lambda p: (p, 0, 0)),
            pl.BlockSpec((2 * window_rows, width), lambda p: (0, 0)),
        ],
        out_specs=pl.BlockSpec((1, n_out, block_count * LANE), lambda p: (p, 0, 0)),
        out_shape=jax.ShapeDtypeStruct((planes, n_out, block_count * LANE), jnp.float32),
        cost_estimate=pl.CostEstimate(
            flops=flops,
            transcendentals=0,
            bytes_accessed=stacked.size * 2 + planes * n_out * block_count * LANE * 4,
        ),
    )(taps, stacked)


def joining(corner, taps, prior, depth_values, window, n_out, bounds, crop, out_shape):
    planes = taps.shape[0]
    group = 16 if planes % 16 == 0 else planes
    _, n_in, width = window.shape
    block_count = width // LANE - 1
    stacked = window.reshape(2 * n_in, width)
    body = functools.partial(
        joining_kernel, n_out=n_out, n_in=n_in, block_count=block_count, bounds=bounds,
        crop=crop,
    )
    out_cols = block_count * LANE
    flops = 2 * planes * (2 * n_out * 2 * n_in * width + block_count * n_out * 4 * LANE * SPAN)
    grid_spec = pltpu.PrefetchScalarGridSpec(
        num_scalar_prefetch=1,
        grid=(planes // group,),
        in_specs=[
            pl.BlockSpec((group, 2, SPAN), lambda p, c: (p, 0, 0)),
            pl.BlockSpec((group, n_out, 1), lambda p, c: (p, 0, 0)),
            pl.BlockSpec((group, 1, 1), lambda p, c: (p, 0, 0)),
            pl.BlockSpec((2 * n_in, width), lambda p, c: (0, 0)),
        ],
        out_specs=[
            pl.BlockSpec(out_shape, lambda p, c: (0, 0)),
            pl.BlockSpec(out_shape, lambda p, c: (0, 0)),
        ],
        scratch_shapes=[pltpu.VMEM((n_out, out_cols), jnp.float32) for _ in range(3)],
    )
    return pl.pallas_call(
        body,
        grid_spec=grid_spec,
        out_shape=[jax.ShapeDtypeStruct(out_shape, jnp.float32)] * 2,
        compiler_params=pltpu.CompilerParams(dimension_semantics=("arbitrary",)),
        cost_estimate=pl.CostEstimate(
            flops=flops,
            transcendentals=0,
            bytes_accessed=stacked.size * 2 + 2 * n_out * out_cols * 4,
        ),
    )(corner, taps, prior, depth_values, stacked)


def gather_depth(block):
    count = lax.axis_size("depth")
    have = 1
    while have < count:
        moved = [
            lax.ppermute(block, "depth", [((j + have * m) % count, j) for j in range(count)])
            for m in range(1, 4)
            if have * m < count
        ]
        block = jnp.concatenate([block, *moved], axis=0)
        have *= 1 + len(moved)
    return block[: count * (block.shape[0] // have)]


def local(hologram, kernel, depth_prior):
    _, rows, col_total = hologram.shape
    local_planes = kernel.shape[0]
    depth_count = lax.axis_size("depth")
    tile_count = lax.axis_size("tile")
    depth_at = lax.axis_index("depth")
    tile_at = lax.axis_index("tile")
    planes_total = local_planes * depth_count
    own_cols = col_total // depth_count
    row_total = rows * tile_count
    half_taps = TAPS // 2

    taps = jnp.pad(kernel.astype(jnp.float32), ((0, 0), (0, 0), (0, SPAN - TAPS)))
    packed = jnp.concatenate([taps.reshape(local_planes, 2 * SPAN), depth_prior], axis=1)
    packed_all = gather_depth(packed)
    owner = (depth_at + jnp.arange(planes_total) // local_planes) % depth_count
    plane_at = owner * local_planes + jnp.arange(planes_total) % local_planes

    halo = 48
    padded = jnp.pad(hologram, ((0, 0), (0, 0), (half_taps, LANE - half_taps)))
    above = lax.ppermute(
        padded[:, rows - halo :], "tile", [(i, i + 1) for i in range(tile_count - 1)]
    )
    below = lax.ppermute(padded[:, :halo], "tile", [(i + 1, i) for i in range(tile_count - 1)])
    extended = jnp.concatenate([above, padded, below], axis=1)

    plane_stack = propagate(taps, extended, rows, halo - half_taps)
    plane_stack, packed_all = lax.optimization_barrier((plane_stack, packed_all))
    taps_all = packed_all[:, : 2 * SPAN].reshape(planes_total, 2, SPAN)
    prior_all = packed_all[:, 2 * SPAN :]

    lead_rows = 8
    n_out = rows + 2 * lead_rows
    first = halo - half_taps - lead_rows
    window = extended[:, first : first + n_out + TAPS - 1, half_taps : half_taps + col_total]
    lead = LANE // 2 + half_taps
    width = own_cols + 2 * LANE
    window = jnp.pad(
        window, ((0, 0), (0, SPAN - window.shape[1]), (lead, width - lead))
    )
    window = lax.dynamic_slice_in_dim(window, depth_at * own_cols, width, axis=2)
    corner = jnp.stack([tile_at * rows - lead_rows, depth_at * own_cols - LANE // 2]).astype(
        jnp.int32
    )
    prior_weight = jnp.exp(prior_all - jnp.max(prior_all, axis=0, keepdims=True))
    prior_rows = jnp.pad(prior_weight, ((0, 0), (lead_rows, lead_rows)), constant_values=1.0)
    depth_values = ((plane_at.astype(jnp.float32) + 0.5) / planes_total)[:, None, None]
    joined, mean_depth = joining(
        corner, taps_all, prior_rows[:, :, None], depth_values, window, n_out,
        (row_total, col_total), (lead_rows, LANE // 2), (rows, own_cols),
    )
    return (plane_stack, joined, mean_depth)


def solution(mesh):
    in_specs = (P(None, "tile", None), P("depth", None, None), P("depth", "tile"))
    out_specs = (P("depth", "tile", None), P("tile", "depth"), P("tile", "depth"))
    return jax.shard_map(local, mesh=mesh, in_specs=in_specs, out_specs=out_specs, check_vma=False)
```

```python
import functools

import jax
import jax.numpy as jnp
from jax import lax
from jax.experimental import pallas as pl
from jax.experimental.pallas import tpu as pltpu
from jax.sharding import PartitionSpec as P

TAPS = 64
LANE = 128
SPAN = 2 * LANE


def skews(taps_ref, plane):
    def skew(taps):
        return pltpu.roll(jnp.broadcast_to(taps, (LANE, SPAN)), 0, 1, stride=1, stride_axis=0)

    return skew(taps_ref[plane, 0:1, :]), skew(taps_ref[plane, 1:2, :])


def rows_matrix(skew_re, skew_im, n_out, n_in):
    rows_re = skew_re[:n_out, :n_in]
    rows_im = skew_im[:n_out, :n_in]
    return jnp.concatenate(
        [
            jnp.concatenate([rows_re, -rows_im], axis=1),
            jnp.concatenate([rows_im, rows_re], axis=1),
        ],
        axis=0,
    ).astype(jnp.bfloat16)


def across_planes(taps_ref, window_ref, n_out, n_in, starts):
    group = taps_ref.shape[0]
    skewed = [skews(taps_ref, g) for g in range(group)]
    matrix = jnp.concatenate([rows_matrix(*sk, n_out, n_in) for sk in skewed], axis=0)
    across = jnp.dot(
        matrix[:, :n_in], window_ref[starts[0] : starts[0] + n_in], preferred_element_type=jnp.float32
    ) + jnp.dot(
        matrix[:, n_in:], window_ref[starts[1] : starts[1] + n_in], preferred_element_type=jnp.float32
    )
    return skewed, across.astype(jnp.bfloat16)


def column_intensity(across, skew_re, skew_im, n_out, block_count):
    across_re = across[:n_out]
    across_im = across[n_out:]

    def stacked(signal, first):
        return jnp.concatenate(
            [signal[:, LANE * b : LANE * (b + 1)] for b in range(first, first + block_count)], axis=0
        )

    blocks = jnp.concatenate(
        [stacked(across_re, 0), stacked(across_re, 1), stacked(across_im, 0), stacked(across_im, 1)],
        axis=1,
    )
    near_re = skew_re[:, :LANE].T
    far_re = skew_re[:, LANE:].T
    near_im = skew_im[:, :LANE].T
    far_im = skew_im[:, LANE:].T
    cols_matrix = jnp.concatenate(
        [
            jnp.concatenate([near_re, near_im], axis=1),
            jnp.concatenate([far_re, far_im], axis=1),
            jnp.concatenate([-near_im, near_re], axis=1),
            jnp.concatenate([-far_im, far_re], axis=1),
        ],
        axis=0,
    ).astype(jnp.bfloat16)
    field = jnp.dot(blocks, cols_matrix, preferred_element_type=jnp.float32)
    return field[:, :LANE] * field[:, :LANE] + field[:, LANE:] * field[:, LANE:]


def propagate_kernel(taps_ref, window_ref, out_ref, *, n_out, n_in, block_count, starts):
    skewed, across = across_planes(taps_ref, window_ref, n_out, n_in, starts)
    for g, (skew_re, skew_im) in enumerate(skewed):
        intensity = column_intensity(
            across[2 * n_out * g : 2 * n_out * (g + 1)], skew_re, skew_im, n_out, block_count
        )
        for b in range(block_count):
            out_ref[g, :, LANE * b : LANE * (b + 1)] = intensity[n_out * b : n_out * (b + 1)]


def joining_kernel(
    corner_ref, taps_ref, prior_ref, depth_ref, window_ref, joined_ref, mean_ref,
    total_ref, weighted_ref, placed_ref, *, n_out, n_in, block_count, bounds, crop, starts,
):
    step = pl.program_id(0)

    @pl.when(step == 0)
    def _():
        total_ref[...] = jnp.zeros(total_ref.shape, jnp.float32)
        weighted_ref[...] = jnp.zeros(weighted_ref.shape, jnp.float32)
        placed_ref[...] = jnp.zeros(placed_ref.shape, jnp.float32)

    skewed, across = across_planes(taps_ref, window_ref, n_out, n_in, starts)
    height, width = n_out, block_count * LANE
    row_at = corner_ref[0] + lax.broadcasted_iota(jnp.int32, (height, width), 0)
    col_at = corner_ref[1] + lax.broadcasted_iota(jnp.int32, (height, width), 1)
    inside = (row_at >= 0) & (row_at < bounds[0]) & (col_at >= 0) & (col_at < bounds[1])
    for g, (skew_re, skew_im) in enumerate(skewed):
        stacked = column_intensity(
            across[2 * n_out * g : 2 * n_out * (g + 1)], skew_re, skew_im, n_out, block_count
        )
        intensity = jnp.concatenate(
            [stacked[n_out * b : n_out * (b + 1)] for b in range(block_count)], axis=1
        )
        intensity = jnp.where(inside, intensity, 0.0)
        vertical = (
            pltpu.roll(intensity, 1, 0) + 2.0 * intensity + pltpu.roll(intensity, height - 1, 0)
        )
        grad_x = pltpu.roll(vertical, width - 1, 1) - pltpu.roll(vertical, 1, 1)
        horizontal = (
            pltpu.roll(intensity, 1, 1) + 2.0 * intensity + pltpu.roll(intensity, width - 1, 1)
        )
        grad_y = pltpu.roll(horizontal, height - 1, 0) - pltpu.roll(horizontal, 1, 0)
        fresh = prior_ref[g] * (1.0 + (grad_x * grad_x + grad_y * grad_y))
        total_ref[...] = total_ref[...] + fresh
        weighted_ref[...] = weighted_ref[...] + fresh * intensity
        placed_ref[...] = placed_ref[...] + fresh * depth_ref[g]

    @pl.when(step == pl.num_programs(0) - 1)
    def _():
        rows, cols = joined_ref.shape
        top, left = crop

        def cropped(values):
            return pltpu.roll(values, width - left, 1)[top : top + rows, :cols]

        joined_ref[...] = cropped(weighted_ref[...] / total_ref[...])
        mean_ref[...] = cropped(placed_ref[...] / total_ref[...])


def propagate(taps, window, n_out, first_row):
    planes = taps.shape[0]
    _, window_rows, width = window.shape
    n_in = n_out + TAPS
    block_count = width // LANE - 1
    stacked = window.reshape(2 * window_rows, width)
    body = functools.partial(
        propagate_kernel, n_out=n_out, n_in=n_in, block_count=block_count,
        starts=(first_row, window_rows + first_row),
    )
    flops = 2 * planes * (2 * n_out * 2 * n_in * width + block_count * n_out * 4 * LANE * SPAN)
    return pl.pallas_call(
        body,
        grid=(planes,),
        in_specs=[
            pl.BlockSpec((1, 2, SPAN), lambda p: (p, 0, 0)),
            pl.BlockSpec((2 * window_rows, width), lambda p: (0, 0)),
        ],
        out_specs=pl.BlockSpec((1, n_out, block_count * LANE), lambda p: (p, 0, 0)),
        out_shape=jax.ShapeDtypeStruct((planes, n_out, block_count * LANE), jnp.float32),
        cost_estimate=pl.CostEstimate(
            flops=flops,
            transcendentals=0,
            bytes_accessed=stacked.size * 2 + planes * n_out * block_count * LANE * 4,
        ),
    )(taps, stacked)


def joining(corner, taps, prior, depth_values, window, n_out, first_row, bounds, crop, out_shape):
    planes = taps.shape[0]
    group = 16 if planes % 16 == 0 else planes
    _, window_rows, width = window.shape
    n_in = SPAN
    block_count = width // LANE - 1
    stacked = window.reshape(2 * window_rows, width)
    body = functools.partial(
        joining_kernel, n_out=n_out, n_in=n_in, block_count=block_count, bounds=bounds,
        crop=crop, starts=(first_row, window_rows + first_row),
    )
    out_cols = block_count * LANE
    flops = 2 * planes * (2 * n_out * 2 * n_in * width + block_count * n_out * 4 * LANE * SPAN)
    grid_spec = pltpu.PrefetchScalarGridSpec(
        num_scalar_prefetch=1,
        grid=(planes // group,),
        in_specs=[
            pl.BlockSpec((group, 2, SPAN), lambda p, c: (p, 0, 0)),
            pl.BlockSpec((group, n_out, 1), lambda p, c: (p, 0, 0)),
            pl.BlockSpec((group, 1, 1), lambda p, c: (p, 0, 0)),
            pl.BlockSpec((2 * window_rows, width), lambda p, c: (0, 0)),
        ],
        out_specs=[
            pl.BlockSpec(out_shape, lambda p, c: (0, 0)),
            pl.BlockSpec(out_shape, lambda p, c: (0, 0)),
        ],
        scratch_shapes=[pltpu.VMEM((n_out, out_cols), jnp.float32) for _ in range(3)],
    )
    return pl.pallas_call(
        body,
        grid_spec=grid_spec,
        out_shape=[jax.ShapeDtypeStruct(out_shape, jnp.float32)] * 2,
        compiler_params=pltpu.CompilerParams(dimension_semantics=("arbitrary",)),
        cost_estimate=pl.CostEstimate(
            flops=flops,
            transcendentals=0,
            bytes_accessed=stacked.size * 2 + 2 * n_out * out_cols * 4,
        ),
    )(corner, taps, prior, depth_values, stacked)


def gather_depth(block):
    count = lax.axis_size("depth")
    have = 1
    while have < count:
        moved = [
            lax.ppermute(block, "depth", [((j + have * m) % count, j) for j in range(count)])
            for m in range(1, 4)
            if have * m < count
        ]
        block = jnp.concatenate([block, *moved], axis=0)
        have *= 1 + len(moved)
    return block[: count * (block.shape[0] // have)]


def local(hologram, kernel, depth_prior):
    _, rows, col_total = hologram.shape
    local_planes = kernel.shape[0]
    depth_count = lax.axis_size("depth")
    tile_count = lax.axis_size("tile")
    depth_at = lax.axis_index("depth")
    tile_at = lax.axis_index("tile")
    planes_total = local_planes * depth_count
    own_cols = col_total // depth_count
    row_total = rows * tile_count
    half_taps = TAPS // 2

    taps = jnp.pad(kernel.astype(jnp.float32), ((0, 0), (0, 0), (0, SPAN - TAPS)))
    packed = jnp.concatenate([taps.reshape(local_planes, 2 * SPAN), depth_prior], axis=1)
    packed_all = gather_depth(packed)
    owner = (depth_at + jnp.arange(planes_total) // local_planes) % depth_count
    plane_at = owner * local_planes + jnp.arange(planes_total) % local_planes

    halo = 48
    padded = jnp.pad(hologram, ((0, 0), (0, 0), (half_taps, LANE - half_taps)))
    above = lax.ppermute(
        padded[:, rows - halo :], "tile", [(i, i + 1) for i in range(tile_count - 1)]
    )
    below = lax.ppermute(padded[:, :halo], "tile", [(i + 1, i) for i in range(tile_count - 1)])
    extended = jnp.concatenate([above, padded, below], axis=1)

    plane_stack = propagate(taps, extended, rows, halo - half_taps)
    plane_stack, packed_all = lax.optimization_barrier((plane_stack, packed_all))
    taps_all = packed_all[:, : 2 * SPAN].reshape(planes_total, 2, SPAN)
    prior_all = packed_all[:, 2 * SPAN :]

    lead_rows = 8
    n_out = rows + 2 * lead_rows
    first = halo - half_taps - lead_rows
    lead = LANE // 2
    width = own_cols + 2 * LANE
    window = jnp.pad(extended, ((0, 0), (0, first + SPAN - extended.shape[1]), (lead, lead)))
    window = lax.dynamic_slice_in_dim(window, depth_at * own_cols, width, axis=2)
    corner = jnp.stack([tile_at * rows - lead_rows, depth_at * own_cols - LANE // 2]).astype(
        jnp.int32
    )
    prior_weight = jnp.exp(prior_all - jnp.max(prior_all, axis=0, keepdims=True))
    prior_rows = jnp.pad(prior_weight, ((0, 0), (lead_rows, lead_rows)), constant_values=1.0)
    depth_values = ((plane_at.astype(jnp.float32) + 0.5) / planes_total)[:, None, None]
    joined, mean_depth = joining(
        corner, taps_all, prior_rows[:, :, None], depth_values, window, n_out, first,
        (row_total, col_total), (lead_rows, LANE // 2), (rows, own_cols),
    )
    return (plane_stack, joined, mean_depth)


def solution(mesh):
    in_specs = (P(None, "tile", None), P("depth", None, None), P("depth", "tile"))
    out_specs = (P("depth", "tile", None), P("tile", "depth"), P("tile", "depth"))
    return jax.shard_map(local, mesh=mesh, in_specs=in_specs, out_specs=out_specs, check_vma=False)
```

```python
import functools

import jax
import jax.numpy as jnp
from jax import lax
from jax.experimental import pallas as pl
from jax.experimental.pallas import tpu as pltpu
from jax.sharding import PartitionSpec as P

TAPS = 64
LANE = 128
SPAN = 2 * LANE


def skews(taps_ref, plane):
    def skew(taps):
        return pltpu.roll(jnp.broadcast_to(taps, (LANE, SPAN)), 0, 1, stride=1, stride_axis=0)

    return skew(taps_ref[plane, 0:1, :]), skew(taps_ref[plane, 1:2, :])


def rows_matrix(skew_re, skew_im, n_out, n_in):
    rows_re = skew_re[:n_out, :n_in]
    rows_im = skew_im[:n_out, :n_in]
    return jnp.concatenate(
        [
            jnp.concatenate([rows_re, -rows_im], axis=1),
            jnp.concatenate([rows_im, rows_re], axis=1),
        ],
        axis=0,
    ).astype(jnp.bfloat16)


def across_planes(taps_ref, window_ref, n_out, n_in, starts):
    group = taps_ref.shape[0]
    skewed = [skews(taps_ref, g) for g in range(group)]
    matrix = jnp.concatenate([rows_matrix(*sk, n_out, n_in) for sk in skewed], axis=0)
    across = jnp.dot(
        matrix[:, :n_in], window_ref[starts[0] : starts[0] + n_in], preferred_element_type=jnp.float32
    ) + jnp.dot(
        matrix[:, n_in:], window_ref[starts[1] : starts[1] + n_in], preferred_element_type=jnp.float32
    )
    return skewed, across.astype(jnp.bfloat16)


def column_intensity(across, skew_re, skew_im, n_out, block_count):
    across_re = across[:n_out]
    across_im = across[n_out:]

    def stacked(signal, first):
        return jnp.concatenate(
            [signal[:, LANE * b : LANE * (b + 1)] for b in range(first, first + block_count)], axis=0
        )

    blocks = jnp.concatenate(
        [stacked(across_re, 0), stacked(across_re, 1), stacked(across_im, 0), stacked(across_im, 1)],
        axis=1,
    )
    near_re = skew_re[:, :LANE].T
    far_re = skew_re[:, LANE:].T
    near_im = skew_im[:, :LANE].T
    far_im = skew_im[:, LANE:].T
    cols_matrix = jnp.concatenate(
        [
            jnp.concatenate([near_re, near_im], axis=1),
            jnp.concatenate([far_re, far_im], axis=1),
            jnp.concatenate([-near_im, near_re], axis=1),
            jnp.concatenate([-far_im, far_re], axis=1),
        ],
        axis=0,
    ).astype(jnp.bfloat16)
    field = jnp.dot(blocks, cols_matrix, preferred_element_type=jnp.float32)
    return field[:, :LANE] * field[:, :LANE] + field[:, LANE:] * field[:, LANE:]


def propagate_kernel(taps_ref, window_ref, out_ref, *, n_out, n_in, block_count, starts):
    skewed, across = across_planes(taps_ref, window_ref, n_out, n_in, starts)
    for g, (skew_re, skew_im) in enumerate(skewed):
        intensity = column_intensity(
            across[2 * n_out * g : 2 * n_out * (g + 1)], skew_re, skew_im, n_out, block_count
        )
        for b in range(block_count):
            out_ref[g, :, LANE * b : LANE * (b + 1)] = intensity[n_out * b : n_out * (b + 1)]


def joining_kernel(
    corner_ref, taps_ref, prior_ref, depth_ref, window_ref, joined_ref, mean_ref,
    total_ref, weighted_ref, placed_ref, *, n_out, n_in, block_count, bounds, crop, starts,
):
    step = pl.program_id(0)

    @pl.when(step == 0)
    def _():
        total_ref[...] = jnp.zeros(total_ref.shape, jnp.float32)
        weighted_ref[...] = jnp.zeros(weighted_ref.shape, jnp.float32)
        placed_ref[...] = jnp.zeros(placed_ref.shape, jnp.float32)

    skewed, across = across_planes(taps_ref, window_ref, n_out, n_in, starts)
    height, width = n_out, block_count * LANE
    row_at = corner_ref[0] + lax.broadcasted_iota(jnp.int32, (height, width), 0)
    col_at = corner_ref[1] + lax.broadcasted_iota(jnp.int32, (height, width), 1)
    inside = (row_at >= 0) & (row_at < bounds[0]) & (col_at >= 0) & (col_at < bounds[1])
    for g, (skew_re, skew_im) in enumerate(skewed):
        stacked = column_intensity(
            across[2 * n_out * g : 2 * n_out * (g + 1)], skew_re, skew_im, n_out, block_count
        )
        intensity = jnp.concatenate(
            [stacked[n_out * b : n_out * (b + 1)] for b in range(block_count)], axis=1
        )
        intensity = jnp.where(inside, intensity, 0.0)
        vertical = (
            pltpu.roll(intensity, 1, 0) + 2.0 * intensity + pltpu.roll(intensity, height - 1, 0)
        )
        grad_x = pltpu.roll(vertical, width - 1, 1) - pltpu.roll(vertical, 1, 1)
        horizontal = (
            pltpu.roll(intensity, 1, 1) + 2.0 * intensity + pltpu.roll(intensity, width - 1, 1)
        )
        grad_y = pltpu.roll(horizontal, height - 1, 0) - pltpu.roll(horizontal, 1, 0)
        fresh = prior_ref[g] * (1.0 + (grad_x * grad_x + grad_y * grad_y))
        total_ref[...] = total_ref[...] + fresh
        weighted_ref[...] = weighted_ref[...] + fresh * intensity
        placed_ref[...] = placed_ref[...] + fresh * depth_ref[g]

    @pl.when(step == pl.num_programs(0) - 1)
    def _():
        rows, cols = joined_ref.shape
        top, left = crop

        def cropped(values):
            return pltpu.roll(values, width - left, 1)[top : top + rows, :cols]

        joined_ref[...] = cropped(weighted_ref[...] / total_ref[...])
        mean_ref[...] = cropped(placed_ref[...] / total_ref[...])


def propagate(taps, window, n_out, first_row):
    planes = taps.shape[0]
    _, window_rows, width = window.shape
    n_in = n_out + TAPS
    block_count = width // LANE - 1
    stacked = window.reshape(2 * window_rows, width)
    body = functools.partial(
        propagate_kernel, n_out=n_out, n_in=n_in, block_count=block_count,
        starts=(first_row, window_rows + first_row),
    )
    flops = 2 * planes * (2 * n_out * 2 * n_in * width + block_count * n_out * 4 * LANE * SPAN)
    return pl.pallas_call(
        body,
        grid=(planes,),
        in_specs=[
            pl.BlockSpec((1, 2, SPAN), lambda p: (p, 0, 0)),
            pl.BlockSpec((2 * window_rows, width), lambda p: (0, 0)),
        ],
        out_specs=pl.BlockSpec((1, n_out, block_count * LANE), lambda p: (p, 0, 0)),
        out_shape=jax.ShapeDtypeStruct((planes, n_out, block_count * LANE), jnp.float32),
        cost_estimate=pl.CostEstimate(
            flops=flops,
            transcendentals=0,
            bytes_accessed=stacked.size * 2 + planes * n_out * block_count * LANE * 4,
        ),
    )(taps, stacked)


def joining(corner, taps, prior, depth_values, window, n_out, first_row, bounds, crop, out_shape):
    planes = taps.shape[0]
    group = 16 if planes % 16 == 0 else planes
    _, window_rows, width = window.shape
    n_in = SPAN
    block_count = width // LANE - 1
    stacked = window.reshape(2 * window_rows, width)
    body = functools.partial(
        joining_kernel, n_out=n_out, n_in=n_in, block_count=block_count, bounds=bounds,
        crop=crop, starts=(first_row, window_rows + first_row),
    )
    out_cols = block_count * LANE
    flops = 2 * planes * (2 * n_out * 2 * n_in * width + block_count * n_out * 4 * LANE * SPAN)
    grid_spec = pltpu.PrefetchScalarGridSpec(
        num_scalar_prefetch=1,
        grid=(planes // group,),
        in_specs=[
            pl.BlockSpec((group, 2, SPAN), lambda p, c: (p, 0, 0)),
            pl.BlockSpec((group, n_out, 1), lambda p, c: (p, 0, 0)),
            pl.BlockSpec((group, 1, 1), lambda p, c: (p, 0, 0)),
            pl.BlockSpec((2 * window_rows, width), lambda p, c: (0, 0)),
        ],
        out_specs=[
            pl.BlockSpec(out_shape, lambda p, c: (0, 0)),
            pl.BlockSpec(out_shape, lambda p, c: (0, 0)),
        ],
        scratch_shapes=[pltpu.VMEM((n_out, out_cols), jnp.float32) for _ in range(3)],
    )
    return pl.pallas_call(
        body,
        grid_spec=grid_spec,
        out_shape=[jax.ShapeDtypeStruct(out_shape, jnp.float32)] * 2,
        compiler_params=pltpu.CompilerParams(dimension_semantics=("arbitrary",)),
        cost_estimate=pl.CostEstimate(
            flops=flops,
            transcendentals=0,
            bytes_accessed=stacked.size * 2 + 2 * n_out * out_cols * 4,
        ),
    )(corner, taps, prior, depth_values, stacked)


def gather_depth(block):
    count = lax.axis_size("depth")
    copies = jnp.broadcast_to(block[None], (count,) + block.shape)
    moved = lax.all_to_all(copies, "depth", 0, 0)
    return moved.reshape(count * block.shape[0], block.shape[1])


def local(hologram, kernel, depth_prior):
    _, rows, col_total = hologram.shape
    local_planes = kernel.shape[0]
    depth_count = lax.axis_size("depth")
    tile_count = lax.axis_size("tile")
    depth_at = lax.axis_index("depth")
    tile_at = lax.axis_index("tile")
    planes_total = local_planes * depth_count
    own_cols = col_total // depth_count
    row_total = rows * tile_count
    half_taps = TAPS // 2

    taps = jnp.pad(kernel.astype(jnp.float32), ((0, 0), (0, 0), (0, SPAN - TAPS)))
    packed = jnp.concatenate([taps.reshape(local_planes, 2 * SPAN), depth_prior], axis=1)
    packed_all = gather_depth(packed)
    plane_at = jnp.arange(planes_total)

    halo = 48
    padded = jnp.pad(hologram, ((0, 0), (0, 0), (half_taps, LANE - half_taps)))
    above = lax.ppermute(
        padded[:, rows - halo :], "tile", [(i, i + 1) for i in range(tile_count - 1)]
    )
    below = lax.ppermute(padded[:, :halo], "tile", [(i + 1, i) for i in range(tile_count - 1)])
    extended = jnp.concatenate([above, padded, below], axis=1)

    plane_stack = propagate(taps, extended, rows, halo - half_taps)
    plane_stack, packed_all = lax.optimization_barrier((plane_stack, packed_all))
    taps_all = packed_all[:, : 2 * SPAN].reshape(planes_total, 2, SPAN)
    prior_all = packed_all[:, 2 * SPAN :]

    lead_rows = 8
    n_out = rows + 2 * lead_rows
    first = halo - half_taps - lead_rows
    lead = LANE // 2
    width = own_cols + 2 * LANE
    window = jnp.pad(extended, ((0, 0), (0, first + SPAN - extended.shape[1]), (lead, lead)))
    window = lax.dynamic_slice_in_dim(window, depth_at * own_cols, width, axis=2)
    corner = jnp.stack([tile_at * rows - lead_rows, depth_at * own_cols - LANE // 2]).astype(
        jnp.int32
    )
    prior_weight = jnp.exp(prior_all - jnp.max(prior_all, axis=0, keepdims=True))
    prior_rows = jnp.pad(prior_weight, ((0, 0), (lead_rows, lead_rows)), constant_values=1.0)
    depth_values = ((plane_at.astype(jnp.float32) + 0.5) / planes_total)[:, None, None]
    joined, mean_depth = joining(
        corner, taps_all, prior_rows[:, :, None], depth_values, window, n_out, first,
        (row_total, col_total), (lead_rows, LANE // 2), (rows, own_cols),
    )
    return (plane_stack, joined, mean_depth)


def solution(mesh):
    in_specs = (P(None, "tile", None), P("depth", None, None), P("depth", "tile"))
    out_specs = (P("depth", "tile", None), P("tile", "depth"), P("tile", "depth"))
    return jax.shard_map(local, mesh=mesh, in_specs=in_specs, out_specs=out_specs, check_vma=False)
```

```python
import functools

import jax
import jax.numpy as jnp
from jax import lax
from jax.experimental import pallas as pl
from jax.experimental.pallas import tpu as pltpu
from jax.sharding import PartitionSpec as P

TAPS = 64
LANE = 128
SPAN = 2 * LANE


def skews(taps_ref, plane):
    def skew(taps):
        return pltpu.roll(jnp.broadcast_to(taps, (LANE, SPAN)), 0, 1, stride=1, stride_axis=0)

    return skew(taps_ref[plane, 0:1, :]), skew(taps_ref[plane, 1:2, :])


def rows_matrix(skew_re, skew_im, n_out, n_in):
    rows_re = skew_re[:n_out, :n_in]
    rows_im = skew_im[:n_out, :n_in]
    return jnp.concatenate(
        [
            jnp.concatenate([rows_re, -rows_im], axis=1),
            jnp.concatenate([rows_im, rows_re], axis=1),
        ],
        axis=0,
    ).astype(jnp.bfloat16)


def across_planes(taps_ref, window_ref, n_out, n_in, starts):
    group = taps_ref.shape[0]
    skewed = [skews(taps_ref, g) for g in range(group)]
    matrix = jnp.concatenate([rows_matrix(*sk, n_out, n_in) for sk in skewed], axis=0)
    across = jnp.dot(
        matrix[:, :n_in], window_ref[starts[0] : starts[0] + n_in], preferred_element_type=jnp.float32
    ) + jnp.dot(
        matrix[:, n_in:], window_ref[starts[1] : starts[1] + n_in], preferred_element_type=jnp.float32
    )
    return skewed, across.astype(jnp.bfloat16)


def column_intensity(across, skew_re, skew_im, n_out, block_count):
    across_re = across[:n_out]
    across_im = across[n_out:]

    def stacked(signal, first):
        return jnp.concatenate(
            [signal[:, LANE * b : LANE * (b + 1)] for b in range(first, first + block_count)], axis=0
        )

    blocks = jnp.concatenate(
        [stacked(across_re, 0), stacked(across_re, 1), stacked(across_im, 0), stacked(across_im, 1)],
        axis=1,
    )
    near_re = skew_re[:, :LANE].T
    far_re = skew_re[:, LANE:].T
    near_im = skew_im[:, :LANE].T
    far_im = skew_im[:, LANE:].T
    cols_matrix = jnp.concatenate(
        [
            jnp.concatenate([near_re, near_im], axis=1),
            jnp.concatenate([far_re, far_im], axis=1),
            jnp.concatenate([-near_im, near_re], axis=1),
            jnp.concatenate([-far_im, far_re], axis=1),
        ],
        axis=0,
    ).astype(jnp.bfloat16)
    field = jnp.dot(blocks, cols_matrix, preferred_element_type=jnp.float32)
    return field[:, :LANE] * field[:, :LANE] + field[:, LANE:] * field[:, LANE:]


def propagate_kernel(taps_ref, window_ref, out_ref, *, n_out, n_in, block_count, starts):
    skewed, across = across_planes(taps_ref, window_ref, n_out, n_in, starts)
    for g, (skew_re, skew_im) in enumerate(skewed):
        intensity = column_intensity(
            across[2 * n_out * g : 2 * n_out * (g + 1)], skew_re, skew_im, n_out, block_count
        )
        for b in range(block_count):
            out_ref[g, :, LANE * b : LANE * (b + 1)] = intensity[n_out * b : n_out * (b + 1)]


def joining_kernel(
    corner_ref, taps_ref, prior_ref, depth_ref, window_ref, joined_ref, mean_ref,
    total_ref, weighted_ref, placed_ref, *, n_out, n_in, block_count, bounds, crop, starts,
):
    step = pl.program_id(0)

    @pl.when(step == 0)
    def _():
        total_ref[...] = jnp.zeros(total_ref.shape, jnp.float32)
        weighted_ref[...] = jnp.zeros(weighted_ref.shape, jnp.float32)
        placed_ref[...] = jnp.zeros(placed_ref.shape, jnp.float32)

    skewed, across = across_planes(taps_ref, window_ref, n_out, n_in, starts)
    height, width = n_out, block_count * LANE
    row_at = corner_ref[0] + lax.broadcasted_iota(jnp.int32, (height, width), 0)
    col_at = corner_ref[1] + lax.broadcasted_iota(jnp.int32, (height, width), 1)
    inside = (row_at >= 0) & (row_at < bounds[0]) & (col_at >= 0) & (col_at < bounds[1])
    for g, (skew_re, skew_im) in enumerate(skewed):
        stacked = column_intensity(
            across[2 * n_out * g : 2 * n_out * (g + 1)], skew_re, skew_im, n_out, block_count
        )
        intensity = jnp.concatenate(
            [stacked[n_out * b : n_out * (b + 1)] for b in range(block_count)], axis=1
        )
        intensity = jnp.where(inside, intensity, 0.0)
        vertical = (
            pltpu.roll(intensity, 1, 0) + 2.0 * intensity + pltpu.roll(intensity, height - 1, 0)
        )
        grad_x = pltpu.roll(vertical, width - 1, 1) - pltpu.roll(vertical, 1, 1)
        horizontal = (
            pltpu.roll(intensity, 1, 1) + 2.0 * intensity + pltpu.roll(intensity, width - 1, 1)
        )
        grad_y = pltpu.roll(horizontal, height - 1, 0) - pltpu.roll(horizontal, 1, 0)
        fresh = prior_ref[g] * (1.0 + (grad_x * grad_x + grad_y * grad_y))
        total_ref[...] = total_ref[...] + fresh
        weighted_ref[...] = weighted_ref[...] + fresh * intensity
        placed_ref[...] = placed_ref[...] + fresh * depth_ref[g]

    @pl.when(step == pl.num_programs(0) - 1)
    def _():
        rows, cols = joined_ref.shape
        top, left = crop

        def cropped(values):
            return pltpu.roll(values, width - left, 1)[top : top + rows, :cols]

        joined_ref[...] = cropped(weighted_ref[...] / total_ref[...])
        mean_ref[...] = cropped(placed_ref[...] / total_ref[...])


def propagate(taps, window, n_out, first_row):
    planes = taps.shape[0]
    _, window_rows, width = window.shape
    n_in = n_out + TAPS
    block_count = width // LANE - 1
    stacked = window.reshape(2 * window_rows, width)
    body = functools.partial(
        propagate_kernel, n_out=n_out, n_in=n_in, block_count=block_count,
        starts=(first_row, window_rows + first_row),
    )
    flops = 2 * planes * (2 * n_out * 2 * n_in * width + block_count * n_out * 4 * LANE * SPAN)
    return pl.pallas_call(
        body,
        grid=(planes,),
        in_specs=[
            pl.BlockSpec((1, 2, SPAN), lambda p: (p, 0, 0)),
            pl.BlockSpec((2 * window_rows, width), lambda p: (0, 0)),
        ],
        out_specs=pl.BlockSpec((1, n_out, block_count * LANE), lambda p: (p, 0, 0)),
        out_shape=jax.ShapeDtypeStruct((planes, n_out, block_count * LANE), jnp.float32),
        cost_estimate=pl.CostEstimate(
            flops=flops,
            transcendentals=0,
            bytes_accessed=stacked.size * 2 + planes * n_out * block_count * LANE * 4,
        ),
    )(taps, stacked)


def joining(corner, taps, prior, depth_values, window, n_out, first_row, bounds, crop, out_shape):
    planes = taps.shape[0]
    group = 16 if planes % 16 == 0 else planes
    _, window_rows, width = window.shape
    n_in = SPAN
    block_count = width // LANE - 1
    stacked = window.reshape(2 * window_rows, width)
    body = functools.partial(
        joining_kernel, n_out=n_out, n_in=n_in, block_count=block_count, bounds=bounds,
        crop=crop, starts=(first_row, window_rows + first_row),
    )
    out_cols = block_count * LANE
    flops = 2 * planes * (2 * n_out * 2 * n_in * width + block_count * n_out * 4 * LANE * SPAN)
    grid_spec = pltpu.PrefetchScalarGridSpec(
        num_scalar_prefetch=1,
        grid=(planes // group,),
        in_specs=[
            pl.BlockSpec((group, 2, SPAN), lambda p, c: (p, 0, 0)),
            pl.BlockSpec((group, n_out, 1), lambda p, c: (p, 0, 0)),
            pl.BlockSpec((group, 1, 1), lambda p, c: (p, 0, 0)),
            pl.BlockSpec((2 * window_rows, width), lambda p, c: (0, 0)),
        ],
        out_specs=[
            pl.BlockSpec(out_shape, lambda p, c: (0, 0)),
            pl.BlockSpec(out_shape, lambda p, c: (0, 0)),
        ],
        scratch_shapes=[pltpu.VMEM((n_out, out_cols), jnp.float32) for _ in range(3)],
    )
    return pl.pallas_call(
        body,
        grid_spec=grid_spec,
        out_shape=[jax.ShapeDtypeStruct(out_shape, jnp.float32)] * 2,
        compiler_params=pltpu.CompilerParams(dimension_semantics=("arbitrary",)),
        cost_estimate=pl.CostEstimate(
            flops=flops,
            transcendentals=0,
            bytes_accessed=stacked.size * 2 + 2 * n_out * out_cols * 4,
        ),
    )(corner, taps, prior, depth_values, stacked)


def gather_depth(block):
    count = lax.axis_size("depth")
    copies = jnp.broadcast_to(block[None], (count,) + block.shape)
    moved = lax.all_to_all(copies, "depth", 0, 0)
    return moved.reshape(count * block.shape[0], block.shape[1])


def local(hologram, kernel, depth_prior):
    _, rows, col_total = hologram.shape
    local_planes = kernel.shape[0]
    depth_count = lax.axis_size("depth")
    tile_count = lax.axis_size("tile")
    depth_at = lax.axis_index("depth")
    tile_at = lax.axis_index("tile")
    planes_total = local_planes * depth_count
    own_cols = col_total // depth_count
    row_total = rows * tile_count
    half_taps = TAPS // 2

    taps = jnp.pad(kernel.astype(jnp.float32), ((0, 0), (0, 0), (0, SPAN - TAPS)))
    packed = jnp.concatenate([taps.reshape(local_planes, 2 * SPAN), depth_prior], axis=1)
    packed_all = gather_depth(packed)
    plane_at = jnp.arange(planes_total)

    halo = 48
    above = lax.ppermute(hologram, "tile", [(i, i + 1) for i in range(tile_count - 1)])
    below = lax.ppermute(hologram, "tile", [(i + 1, i) for i in range(tile_count - 1)])
    extended = jnp.concatenate([above[:, rows - halo :], hologram, below[:, :halo]], axis=1)
    extended = jnp.pad(extended, ((0, 0), (0, 0), (half_taps, LANE - half_taps)))

    plane_stack = propagate(taps, extended, rows, halo - half_taps)
    plane_stack, packed_all = lax.optimization_barrier((plane_stack, packed_all))
    taps_all = packed_all[:, : 2 * SPAN].reshape(planes_total, 2, SPAN)
    prior_all = packed_all[:, 2 * SPAN :]

    lead_rows = 8
    n_out = rows + 2 * lead_rows
    first = halo - half_taps - lead_rows
    lead = LANE // 2
    width = own_cols + 2 * LANE
    window = jnp.pad(extended, ((0, 0), (0, first + SPAN - extended.shape[1]), (lead, lead)))
    window = lax.dynamic_slice_in_dim(window, depth_at * own_cols, width, axis=2)
    corner = jnp.stack([tile_at * rows - lead_rows, depth_at * own_cols - LANE // 2]).astype(
        jnp.int32
    )
    prior_weight = jnp.exp(prior_all - jnp.max(prior_all, axis=0, keepdims=True))
    prior_rows = jnp.pad(prior_weight, ((0, 0), (lead_rows, lead_rows)), constant_values=1.0)
    depth_values = ((plane_at.astype(jnp.float32) + 0.5) / planes_total)[:, None, None]
    joined, mean_depth = joining(
        corner, taps_all, prior_rows[:, :, None], depth_values, window, n_out, first,
        (row_total, col_total), (lead_rows, LANE // 2), (rows, own_cols),
    )
    return (plane_stack, joined, mean_depth)


def solution(mesh):
    in_specs = (P(None, "tile", None), P("depth", None, None), P("depth", "tile"))
    out_specs = (P("depth", "tile", None), P("tile", "depth"), P("tile", "depth"))
    return jax.shard_map(local, mesh=mesh, in_specs=in_specs, out_specs=out_specs, check_vma=False)
```

```python
import functools

import jax
import jax.numpy as jnp
from jax import lax
from jax.experimental import pallas as pl
from jax.experimental.pallas import tpu as pltpu
from jax.sharding import PartitionSpec as P

TAPS = 64
LANE = 128
SPAN = 2 * LANE


def skews(taps_ref, plane):
    def skew(taps):
        return pltpu.roll(jnp.broadcast_to(taps, (LANE, SPAN)), 0, 1, stride=1, stride_axis=0)

    if len(taps_ref.shape) == 3:
        return skew(taps_ref[plane, 0:1, :]), skew(taps_ref[plane, 1:2, :])
    row = taps_ref[plane : plane + 1]
    return skew(row[:, :SPAN]), skew(row[:, SPAN : 2 * SPAN])


def rows_matrix(skew_re, skew_im, n_out, n_in):
    rows_re = skew_re[:n_out, :n_in]
    rows_im = skew_im[:n_out, :n_in]
    return jnp.concatenate(
        [
            jnp.concatenate([rows_re, -rows_im], axis=1),
            jnp.concatenate([rows_im, rows_re], axis=1),
        ],
        axis=0,
    ).astype(jnp.bfloat16)


def across_planes(taps_ref, window_ref, n_out, n_in, starts):
    group = taps_ref.shape[0]
    skewed = [skews(taps_ref, g) for g in range(group)]
    matrix = jnp.concatenate([rows_matrix(*sk, n_out, n_in) for sk in skewed], axis=0)
    across = jnp.dot(
        matrix[:, :n_in], window_ref[starts[0] : starts[0] + n_in], preferred_element_type=jnp.float32
    ) + jnp.dot(
        matrix[:, n_in:], window_ref[starts[1] : starts[1] + n_in], preferred_element_type=jnp.float32
    )
    return skewed, across.astype(jnp.bfloat16)


def column_intensity(across, skew_re, skew_im, n_out, block_count):
    across_re = across[:n_out]
    across_im = across[n_out:]

    def stacked(signal, first):
        return jnp.concatenate(
            [signal[:, LANE * b : LANE * (b + 1)] for b in range(first, first + block_count)], axis=0
        )

    blocks = jnp.concatenate(
        [stacked(across_re, 0), stacked(across_re, 1), stacked(across_im, 0), stacked(across_im, 1)],
        axis=1,
    )
    near_re = skew_re[:, :LANE].T
    far_re = skew_re[:, LANE:].T
    near_im = skew_im[:, :LANE].T
    far_im = skew_im[:, LANE:].T
    cols_matrix = jnp.concatenate(
        [
            jnp.concatenate([near_re, near_im], axis=1),
            jnp.concatenate([far_re, far_im], axis=1),
            jnp.concatenate([-near_im, near_re], axis=1),
            jnp.concatenate([-far_im, far_re], axis=1),
        ],
        axis=0,
    ).astype(jnp.bfloat16)
    field = jnp.dot(blocks, cols_matrix, preferred_element_type=jnp.float32)
    return field[:, :LANE] * field[:, :LANE] + field[:, LANE:] * field[:, LANE:]


def propagate_kernel(taps_ref, window_ref, out_ref, *, n_out, n_in, block_count, starts):
    skewed, across = across_planes(taps_ref, window_ref, n_out, n_in, starts)
    for g, (skew_re, skew_im) in enumerate(skewed):
        intensity = column_intensity(
            across[2 * n_out * g : 2 * n_out * (g + 1)], skew_re, skew_im, n_out, block_count
        )
        for b in range(block_count):
            out_ref[g, :, LANE * b : LANE * (b + 1)] = intensity[n_out * b : n_out * (b + 1)]


def joining_kernel(
    corner_ref, taps_ref, prior_ref, depth_ref, window_ref, joined_ref, mean_ref,
    total_ref, weighted_ref, placed_ref, *, n_out, n_in, block_count, bounds, crop, starts,
):
    step = pl.program_id(0)

    @pl.when(step == 0)
    def _():
        total_ref[...] = jnp.zeros(total_ref.shape, jnp.float32)
        weighted_ref[...] = jnp.zeros(weighted_ref.shape, jnp.float32)
        placed_ref[...] = jnp.zeros(placed_ref.shape, jnp.float32)

    skewed, across = across_planes(taps_ref, window_ref, n_out, n_in, starts)
    height, width = n_out, block_count * LANE
    row_at = corner_ref[0] + lax.broadcasted_iota(jnp.int32, (height, width), 0)
    col_at = corner_ref[1] + lax.broadcasted_iota(jnp.int32, (height, width), 1)
    inside = (row_at >= 0) & (row_at < bounds[0]) & (col_at >= 0) & (col_at < bounds[1])
    for g, (skew_re, skew_im) in enumerate(skewed):
        stacked = column_intensity(
            across[2 * n_out * g : 2 * n_out * (g + 1)], skew_re, skew_im, n_out, block_count
        )
        intensity = jnp.concatenate(
            [stacked[n_out * b : n_out * (b + 1)] for b in range(block_count)], axis=1
        )
        intensity = jnp.where(inside, intensity, 0.0)
        vertical = (
            pltpu.roll(intensity, 1, 0) + 2.0 * intensity + pltpu.roll(intensity, height - 1, 0)
        )
        grad_x = pltpu.roll(vertical, width - 1, 1) - pltpu.roll(vertical, 1, 1)
        horizontal = (
            pltpu.roll(intensity, 1, 1) + 2.0 * intensity + pltpu.roll(intensity, width - 1, 1)
        )
        grad_y = pltpu.roll(horizontal, height - 1, 0) - pltpu.roll(horizontal, 1, 0)
        fresh = prior_ref[g][:, 0:1] * (1.0 + (grad_x * grad_x + grad_y * grad_y))
        total_ref[...] = total_ref[...] + fresh
        weighted_ref[...] = weighted_ref[...] + fresh * intensity
        placed_ref[...] = placed_ref[...] + fresh * depth_ref[g]

    @pl.when(step == pl.num_programs(0) - 1)
    def _():
        rows, cols = joined_ref.shape
        top, left = crop

        def cropped(values):
            return pltpu.roll(values, width - left, 1)[top : top + rows, :cols]

        joined_ref[...] = cropped(weighted_ref[...] / total_ref[...])
        mean_ref[...] = cropped(placed_ref[...] / total_ref[...])


def propagate(taps, window, n_out, first_row):
    planes = taps.shape[0]
    _, window_rows, width = window.shape
    n_in = n_out + TAPS
    block_count = width // LANE - 1
    stacked = window.reshape(2 * window_rows, width)
    body = functools.partial(
        propagate_kernel, n_out=n_out, n_in=n_in, block_count=block_count,
        starts=(first_row, window_rows + first_row),
    )
    flops = 2 * planes * (2 * n_out * 2 * n_in * width + block_count * n_out * 4 * LANE * SPAN)
    return pl.pallas_call(
        body,
        grid=(planes,),
        in_specs=[
            pl.BlockSpec((1, 2, SPAN), lambda p: (p, 0, 0)),
            pl.BlockSpec((2 * window_rows, width), lambda p: (0, 0)),
        ],
        out_specs=pl.BlockSpec((1, n_out, block_count * LANE), lambda p: (p, 0, 0)),
        out_shape=jax.ShapeDtypeStruct((planes, n_out, block_count * LANE), jnp.float32),
        cost_estimate=pl.CostEstimate(
            flops=flops,
            transcendentals=0,
            bytes_accessed=stacked.size * 2 + planes * n_out * block_count * LANE * 4,
        ),
    )(taps, stacked)


def joining(corner, taps, prior, depth_values, window, n_out, first_row, bounds, crop, out_shape):
    planes = taps.shape[0]
    group = 16 if planes % 16 == 0 else planes
    _, window_rows, width = window.shape
    n_in = SPAN
    block_count = width // LANE - 1
    stacked = window.reshape(2 * window_rows, width)
    body = functools.partial(
        joining_kernel, n_out=n_out, n_in=n_in, block_count=block_count, bounds=bounds,
        crop=crop, starts=(first_row, window_rows + first_row),
    )
    out_cols = block_count * LANE
    flops = 2 * planes * (2 * n_out * 2 * n_in * width + block_count * n_out * 4 * LANE * SPAN)
    grid_spec = pltpu.PrefetchScalarGridSpec(
        num_scalar_prefetch=1,
        grid=(planes // group,),
        in_specs=[
            pl.BlockSpec((group, taps.shape[1]), lambda p, c: (p, 0)),
            pl.BlockSpec((group, n_out, LANE), lambda p, c: (p, 0, 0)),
            pl.BlockSpec((group, 1, 1), lambda p, c: (p, 0, 0)),
            pl.BlockSpec((2 * window_rows, width), lambda p, c: (0, 0)),
        ],
        out_specs=[
            pl.BlockSpec(out_shape, lambda p, c: (0, 0)),
            pl.BlockSpec(out_shape, lambda p, c: (0, 0)),
        ],
        scratch_shapes=[pltpu.VMEM((n_out, out_cols), jnp.float32) for _ in range(3)],
    )
    return pl.pallas_call(
        body,
        grid_spec=grid_spec,
        out_shape=[jax.ShapeDtypeStruct(out_shape, jnp.float32)] * 2,
        compiler_params=pltpu.CompilerParams(dimension_semantics=("arbitrary",)),
        cost_estimate=pl.CostEstimate(
            flops=flops,
            transcendentals=0,
            bytes_accessed=stacked.size * 2 + 2 * n_out * out_cols * 4,
        ),
    )(corner, taps, prior, depth_values, stacked)


def gather_depth(block):
    count = lax.axis_size("depth")
    copies = jnp.broadcast_to(block[None], (count,) + block.shape)
    moved = lax.all_to_all(copies, "depth", 0, 0)
    return moved.reshape(count * block.shape[0], block.shape[1])


def local(hologram, kernel, depth_prior):
    _, rows, col_total = hologram.shape
    local_planes = kernel.shape[0]
    depth_count = lax.axis_size("depth")
    tile_count = lax.axis_size("tile")
    depth_at = lax.axis_index("depth")
    tile_at = lax.axis_index("tile")
    planes_total = local_planes * depth_count
    own_cols = col_total // depth_count
    row_total = rows * tile_count
    half_taps = TAPS // 2

    taps = jnp.pad(kernel.astype(jnp.float32), ((0, 0), (0, 0), (0, SPAN - TAPS)))
    packed = jnp.concatenate([taps.reshape(local_planes, 2 * SPAN), depth_prior], axis=1)
    packed_all = gather_depth(packed)
    plane_at = jnp.arange(planes_total)

    halo = 48
    above = lax.ppermute(hologram, "tile", [(i, i + 1) for i in range(tile_count - 1)])
    below = lax.ppermute(hologram, "tile", [(i + 1, i) for i in range(tile_count - 1)])
    extended = jnp.concatenate([above[:, rows - halo :], hologram, below[:, :halo]], axis=1)
    extended = jnp.pad(extended, ((0, 0), (0, 0), (half_taps, LANE - half_taps)))

    plane_stack = propagate(taps, extended, rows, halo - half_taps)
    plane_stack, packed_all = lax.optimization_barrier((plane_stack, packed_all))
    prior_all = packed_all[:, 2 * SPAN :]

    lead_rows = 8
    n_out = rows + 2 * lead_rows
    first = halo - half_taps - lead_rows
    lead = LANE // 2
    width = own_cols + 2 * LANE
    window = jnp.pad(extended, ((0, 0), (0, first + SPAN - extended.shape[1]), (lead, lead)))
    window = lax.dynamic_slice_in_dim(window, depth_at * own_cols, width, axis=2)
    corner = jnp.stack([tile_at * rows - lead_rows, depth_at * own_cols - LANE // 2]).astype(
        jnp.int32
    )
    prior_weight = jnp.exp(prior_all - jnp.max(prior_all, axis=0, keepdims=True))
    prior_rows = jnp.pad(prior_weight, ((0, 0), (lead_rows, lead_rows)), constant_values=1.0)
    depth_values = ((plane_at.astype(jnp.float32) + 0.5) / planes_total)[:, None, None]
    joined, mean_depth = joining(
        corner, packed_all, jnp.broadcast_to(prior_rows[:, :, None], prior_rows.shape + (LANE,)),
        depth_values, window, n_out, first,
        (row_total, col_total), (lead_rows, LANE // 2), (rows, own_cols),
    )
    return (plane_stack, joined, mean_depth)


def solution(mesh):
    in_specs = (P(None, "tile", None), P("depth", None, None), P("depth", "tile"))
    out_specs = (P("depth", "tile", None), P("tile", "depth"), P("tile", "depth"))
    return jax.shard_map(local, mesh=mesh, in_specs=in_specs, out_specs=out_specs, check_vma=False)
```

```python
import functools

import jax
import jax.numpy as jnp
from jax import lax
from jax.experimental import pallas as pl
from jax.experimental.pallas import tpu as pltpu
from jax.sharding import PartitionSpec as P

TAPS = 64
LANE = 128
SPAN = 2 * LANE


def skews(taps_ref, plane):
    def skew(taps):
        return pltpu.roll(jnp.broadcast_to(taps, (LANE, SPAN)), 0, 1, stride=1, stride_axis=0)

    if len(taps_ref.shape) == 3:
        return skew(taps_ref[plane, 0:1, :]), skew(taps_ref[plane, 1:2, :])
    row = taps_ref[plane : plane + 1]
    return skew(row[:, :SPAN]), skew(row[:, SPAN : 2 * SPAN])


def rows_matrix(skew_re, skew_im, n_out, n_in):
    rows_re = skew_re[:n_out, :n_in]
    rows_im = skew_im[:n_out, :n_in]
    return jnp.concatenate(
        [
            jnp.concatenate([rows_re, -rows_im], axis=1),
            jnp.concatenate([rows_im, rows_re], axis=1),
        ],
        axis=0,
    ).astype(jnp.bfloat16)


def across_planes(taps_ref, window_ref, n_out, n_in, starts):
    group = taps_ref.shape[0]
    skewed = [skews(taps_ref, g) for g in range(group)]
    matrix = jnp.concatenate([rows_matrix(*sk, n_out, n_in) for sk in skewed], axis=0)
    across = jnp.dot(
        matrix[:, :n_in], window_ref[starts[0] : starts[0] + n_in], preferred_element_type=jnp.float32
    ) + jnp.dot(
        matrix[:, n_in:], window_ref[starts[1] : starts[1] + n_in], preferred_element_type=jnp.float32
    )
    return skewed, across.astype(jnp.bfloat16)


def column_intensity(across, skew_re, skew_im, n_out, block_count):
    across_re = across[:n_out]
    across_im = across[n_out:]

    def stacked(signal, first):
        return jnp.concatenate(
            [signal[:, LANE * b : LANE * (b + 1)] for b in range(first, first + block_count)], axis=0
        )

    blocks = jnp.concatenate(
        [stacked(across_re, 0), stacked(across_re, 1), stacked(across_im, 0), stacked(across_im, 1)],
        axis=1,
    )
    near_re = skew_re[:, :LANE].T
    far_re = skew_re[:, LANE:].T
    near_im = skew_im[:, :LANE].T
    far_im = skew_im[:, LANE:].T
    cols_matrix = jnp.concatenate(
        [
            jnp.concatenate([near_re, near_im], axis=1),
            jnp.concatenate([far_re, far_im], axis=1),
            jnp.concatenate([-near_im, near_re], axis=1),
            jnp.concatenate([-far_im, far_re], axis=1),
        ],
        axis=0,
    ).astype(jnp.bfloat16)
    field = jnp.dot(blocks, cols_matrix, preferred_element_type=jnp.float32)
    return field[:, :LANE] * field[:, :LANE] + field[:, LANE:] * field[:, LANE:]


def propagate_kernel(taps_ref, window_ref, out_ref, *, n_out, n_in, block_count, starts):
    skewed, across = across_planes(taps_ref, window_ref, n_out, n_in, starts)
    for g, (skew_re, skew_im) in enumerate(skewed):
        intensity = column_intensity(
            across[2 * n_out * g : 2 * n_out * (g + 1)], skew_re, skew_im, n_out, block_count
        )
        for b in range(block_count):
            out_ref[g, :, LANE * b : LANE * (b + 1)] = intensity[n_out * b : n_out * (b + 1)]


def joining_kernel(
    corner_ref, taps_ref, prior_ref, depth_ref, window_ref, joined_ref, mean_ref,
    total_ref, weighted_ref, placed_ref, *, n_out, n_in, block_count, bounds, crop, starts,
):
    step = pl.program_id(0)

    @pl.when(step == 0)
    def _():
        total_ref[...] = jnp.zeros(total_ref.shape, jnp.float32)
        weighted_ref[...] = jnp.zeros(weighted_ref.shape, jnp.float32)
        placed_ref[...] = jnp.zeros(placed_ref.shape, jnp.float32)

    skewed, across = across_planes(taps_ref, window_ref, n_out, n_in, starts)
    height, width = n_out, block_count * LANE
    row_at = corner_ref[0] + lax.broadcasted_iota(jnp.int32, (height, width), 0)
    col_at = corner_ref[1] + lax.broadcasted_iota(jnp.int32, (height, width), 1)
    inside = (row_at >= 0) & (row_at < bounds[0]) & (col_at >= 0) & (col_at < bounds[1])
    for g, (skew_re, skew_im) in enumerate(skewed):
        stacked = column_intensity(
            across[2 * n_out * g : 2 * n_out * (g + 1)], skew_re, skew_im, n_out, block_count
        )
        intensity = jnp.concatenate(
            [stacked[n_out * b : n_out * (b + 1)] for b in range(block_count)], axis=1
        )
        intensity = jnp.where(inside, intensity, 0.0)
        vertical = (
            pltpu.roll(intensity, 1, 0) + 2.0 * intensity + pltpu.roll(intensity, height - 1, 0)
        )
        grad_x = pltpu.roll(vertical, width - 1, 1) - pltpu.roll(vertical, 1, 1)
        horizontal = (
            pltpu.roll(intensity, 1, 1) + 2.0 * intensity + pltpu.roll(intensity, width - 1, 1)
        )
        grad_y = pltpu.roll(horizontal, height - 1, 0) - pltpu.roll(horizontal, 1, 0)
        fresh = prior_ref[g][:, 0:1] * (1.0 + (grad_x * grad_x + grad_y * grad_y))
        total_ref[...] = total_ref[...] + fresh
        weighted_ref[...] = weighted_ref[...] + fresh * intensity
        placed_ref[...] = placed_ref[...] + fresh * depth_ref[g]

    @pl.when(step == pl.num_programs(0) - 1)
    def _():
        rows, cols = joined_ref.shape
        top, left = crop

        def cropped(values):
            return pltpu.roll(values, width - left, 1)[top : top + rows, :cols]

        joined_ref[...] = cropped(weighted_ref[...] / total_ref[...])
        mean_ref[...] = cropped(placed_ref[...] / total_ref[...])


def propagate(taps, window, n_out, first_row):
    planes = taps.shape[0]
    _, window_rows, width = window.shape
    n_in = n_out + TAPS
    block_count = width // LANE - 1
    stacked = window.reshape(2 * window_rows, width)
    body = functools.partial(
        propagate_kernel, n_out=n_out, n_in=n_in, block_count=block_count,
        starts=(first_row, window_rows + first_row),
    )
    flops = 2 * planes * (2 * n_out * 2 * n_in * width + block_count * n_out * 4 * LANE * SPAN)
    return pl.pallas_call(
        body,
        grid=(planes,),
        in_specs=[
            pl.BlockSpec((1, 2, SPAN), lambda p: (p, 0, 0)),
            pl.BlockSpec((2 * window_rows, width), lambda p: (0, 0)),
        ],
        out_specs=pl.BlockSpec((1, n_out, block_count * LANE), lambda p: (p, 0, 0)),
        out_shape=jax.ShapeDtypeStruct((planes, n_out, block_count * LANE), jnp.float32),
        cost_estimate=pl.CostEstimate(
            flops=flops,
            transcendentals=0,
            bytes_accessed=stacked.size * 2 + planes * n_out * block_count * LANE * 4,
        ),
    )(taps, stacked)


def joining(corner, taps, prior, depth_values, window, n_out, first_row, bounds, crop, out_shape):
    planes = taps.shape[0]
    group = 32 if planes % 32 == 0 else planes
    _, window_rows, width = window.shape
    n_in = SPAN
    block_count = width // LANE - 1
    stacked = window.reshape(2 * window_rows, width)
    body = functools.partial(
        joining_kernel, n_out=n_out, n_in=n_in, block_count=block_count, bounds=bounds,
        crop=crop, starts=(first_row, window_rows + first_row),
    )
    out_cols = block_count * LANE
    flops = 2 * planes * (2 * n_out * 2 * n_in * width + block_count * n_out * 4 * LANE * SPAN)
    grid_spec = pltpu.PrefetchScalarGridSpec(
        num_scalar_prefetch=1,
        grid=(planes // group,),
        in_specs=[
            pl.BlockSpec((group, taps.shape[1]), lambda p, c: (p, 0)),
            pl.BlockSpec((group, n_out, LANE), lambda p, c: (p, 0, 0)),
            pl.BlockSpec((group, 1, 1), lambda p, c: (p, 0, 0)),
            pl.BlockSpec((2 * window_rows, width), lambda p, c: (0, 0)),
        ],
        out_specs=[
            pl.BlockSpec(out_shape, lambda p, c: (0, 0)),
            pl.BlockSpec(out_shape, lambda p, c: (0, 0)),
        ],
        scratch_shapes=[pltpu.VMEM((n_out, out_cols), jnp.float32) for _ in range(3)],
    )
    return pl.pallas_call(
        body,
        grid_spec=grid_spec,
        out_shape=[jax.ShapeDtypeStruct(out_shape, jnp.float32)] * 2,
        compiler_params=pltpu.CompilerParams(dimension_semantics=("arbitrary",)),
        cost_estimate=pl.CostEstimate(
            flops=flops,
            transcendentals=0,
            bytes_accessed=stacked.size * 2 + 2 * n_out * out_cols * 4,
        ),
    )(corner, taps, prior, depth_values, stacked)


def gather_depth(block):
    count = lax.axis_size("depth")
    copies = jnp.broadcast_to(block[None], (count,) + block.shape)
    moved = lax.all_to_all(copies, "depth", 0, 0)
    return moved.reshape(count * block.shape[0], block.shape[1])


def local(hologram, kernel, depth_prior):
    _, rows, col_total = hologram.shape
    local_planes = kernel.shape[0]
    depth_count = lax.axis_size("depth")
    tile_count = lax.axis_size("tile")
    depth_at = lax.axis_index("depth")
    tile_at = lax.axis_index("tile")
    planes_total = local_planes * depth_count
    own_cols = col_total // depth_count
    row_total = rows * tile_count
    half_taps = TAPS // 2

    taps = jnp.pad(kernel.astype(jnp.float32), ((0, 0), (0, 0), (0, SPAN - TAPS)))
    packed = jnp.concatenate([taps.reshape(local_planes, 2 * SPAN), depth_prior], axis=1)
    packed_all = gather_depth(packed)
    plane_at = jnp.arange(planes_total)

    halo = 48
    above = lax.ppermute(hologram, "tile", [(i, i + 1) for i in range(tile_count - 1)])
    below = lax.ppermute(hologram, "tile", [(i + 1, i) for i in range(tile_count - 1)])
    extended = jnp.concatenate([above[:, rows - halo :], hologram, below[:, :halo]], axis=1)
    extended = jnp.pad(extended, ((0, 0), (0, 0), (half_taps, LANE - half_taps)))

    plane_stack = propagate(taps, extended, rows, halo - half_taps)
    plane_stack, packed_all = lax.optimization_barrier((plane_stack, packed_all))
    prior_all = packed_all[:, 2 * SPAN :]

    lead_rows = 8
    n_out = rows + 2 * lead_rows
    first = halo - half_taps - lead_rows
    lead = LANE // 2
    width = own_cols + 2 * LANE
    window = jnp.pad(extended, ((0, 0), (0, first + SPAN - extended.shape[1]), (lead, lead)))
    window = lax.dynamic_slice_in_dim(window, depth_at * own_cols, width, axis=2)
    corner = jnp.stack([tile_at * rows - lead_rows, depth_at * own_cols - LANE // 2]).astype(
        jnp.int32
    )
    prior_weight = jnp.exp(prior_all - jnp.max(prior_all, axis=0, keepdims=True))
    prior_rows = jnp.pad(prior_weight, ((0, 0), (lead_rows, lead_rows)), constant_values=1.0)
    depth_values = ((plane_at.astype(jnp.float32) + 0.5) / planes_total)[:, None, None]
    joined, mean_depth = joining(
        corner, packed_all, jnp.broadcast_to(prior_rows[:, :, None], prior_rows.shape + (LANE,)),
        depth_values, window, n_out, first,
        (row_total, col_total), (lead_rows, LANE // 2), (rows, own_cols),
    )
    return (plane_stack, joined, mean_depth)


def solution(mesh):
    in_specs = (P(None, "tile", None), P("depth", None, None), P("depth", "tile"))
    out_specs = (P("depth", "tile", None), P("tile", "depth"), P("tile", "depth"))
    return jax.shard_map(local, mesh=mesh, in_specs=in_specs, out_specs=out_specs, check_vma=False)
```

```python
import functools

import jax
import jax.numpy as jnp
from jax import lax
from jax.experimental import pallas as pl
from jax.experimental.pallas import tpu as pltpu
from jax.sharding import PartitionSpec as P

TAPS = 64
LANE = 128
SPAN = 2 * LANE


def skews(taps_ref, plane):
    def skew(taps):
        return pltpu.roll(jnp.broadcast_to(taps, (LANE, SPAN)), 0, 1, stride=1, stride_axis=0)

    if len(taps_ref.shape) == 3:
        return skew(taps_ref[plane, 0:1, :]), skew(taps_ref[plane, 1:2, :])
    row = taps_ref[plane : plane + 1]
    return skew(row[:, :SPAN]), skew(row[:, SPAN : 2 * SPAN])


def rows_matrix(skew_re, skew_im, n_out, n_in):
    rows_re = skew_re[:n_out, :n_in]
    rows_im = skew_im[:n_out, :n_in]
    return jnp.concatenate(
        [
            jnp.concatenate([rows_re, -rows_im], axis=1),
            jnp.concatenate([rows_im, rows_re], axis=1),
        ],
        axis=0,
    ).astype(jnp.bfloat16)


def across_planes(taps_ref, window_ref, n_out, n_in, starts):
    group = taps_ref.shape[0]
    skewed = [skews(taps_ref, g) for g in range(group)]
    matrix = jnp.concatenate([rows_matrix(*sk, n_out, n_in) for sk in skewed], axis=0)
    across = jnp.dot(
        matrix[:, :n_in], window_ref[starts[0] : starts[0] + n_in], preferred_element_type=jnp.float32
    ) + jnp.dot(
        matrix[:, n_in:], window_ref[starts[1] : starts[1] + n_in], preferred_element_type=jnp.float32
    )
    return skewed, across.astype(jnp.bfloat16)


def column_intensity(across, skew_re, skew_im, n_out, block_count):
    across_re = across[:n_out]
    across_im = across[n_out:]

    def stacked(signal, first):
        return jnp.concatenate(
            [signal[:, LANE * b : LANE * (b + 1)] for b in range(first, first + block_count)], axis=0
        )

    blocks = jnp.concatenate(
        [stacked(across_re, 0), stacked(across_re, 1), stacked(across_im, 0), stacked(across_im, 1)],
        axis=1,
    )
    near_re = skew_re[:, :LANE].T
    far_re = skew_re[:, LANE:].T
    near_im = skew_im[:, :LANE].T
    far_im = skew_im[:, LANE:].T
    cols_matrix = jnp.concatenate(
        [
            jnp.concatenate([near_re, near_im], axis=1),
            jnp.concatenate([far_re, far_im], axis=1),
            jnp.concatenate([-near_im, near_re], axis=1),
            jnp.concatenate([-far_im, far_re], axis=1),
        ],
        axis=0,
    ).astype(jnp.bfloat16)
    field = jnp.dot(blocks, cols_matrix, preferred_element_type=jnp.float32)
    return field[:, :LANE] * field[:, :LANE] + field[:, LANE:] * field[:, LANE:]


def propagate_kernel(taps_ref, window_ref, out_ref, *, n_out, n_in, block_count, starts):
    skewed, across = across_planes(taps_ref, window_ref, n_out, n_in, starts)
    for g, (skew_re, skew_im) in enumerate(skewed):
        intensity = column_intensity(
            across[2 * n_out * g : 2 * n_out * (g + 1)], skew_re, skew_im, n_out, block_count
        )
        for b in range(block_count):
            out_ref[g, :, LANE * b : LANE * (b + 1)] = intensity[n_out * b : n_out * (b + 1)]


def joining_kernel(
    corner_ref, taps_ref, prior_ref, window_ref, joined_ref, mean_ref,
    total_ref, weighted_ref, placed_ref, *, n_out, n_in, block_count, bounds, crop, starts,
):
    step = pl.program_id(0)

    @pl.when(step == 0)
    def _():
        total_ref[...] = jnp.zeros(total_ref.shape, jnp.float32)
        weighted_ref[...] = jnp.zeros(weighted_ref.shape, jnp.float32)
        placed_ref[...] = jnp.zeros(placed_ref.shape, jnp.float32)

    skewed, across = across_planes(taps_ref, window_ref, n_out, n_in, starts)
    height, width = n_out, block_count * LANE
    row_at = corner_ref[0] + lax.broadcasted_iota(jnp.int32, (height, width), 0)
    col_at = corner_ref[1] + lax.broadcasted_iota(jnp.int32, (height, width), 1)
    inside = (row_at >= 0) & (row_at < bounds[0]) & (col_at >= 0) & (col_at < bounds[1])
    for g, (skew_re, skew_im) in enumerate(skewed):
        stacked = column_intensity(
            across[2 * n_out * g : 2 * n_out * (g + 1)], skew_re, skew_im, n_out, block_count
        )
        intensity = jnp.concatenate(
            [stacked[n_out * b : n_out * (b + 1)] for b in range(block_count)], axis=1
        )
        intensity = jnp.where(inside, intensity, 0.0)
        vertical = (
            pltpu.roll(intensity, 1, 0) + 2.0 * intensity + pltpu.roll(intensity, height - 1, 0)
        )
        grad_x = pltpu.roll(vertical, width - 1, 1) - pltpu.roll(vertical, 1, 1)
        horizontal = (
            pltpu.roll(intensity, 1, 1) + 2.0 * intensity + pltpu.roll(intensity, width - 1, 1)
        )
        grad_y = pltpu.roll(horizontal, height - 1, 0) - pltpu.roll(horizontal, 1, 0)
        fresh = prior_ref[g][:, 0:1] * (1.0 + (grad_x * grad_x + grad_y * grad_y))
        total_ref[...] = total_ref[...] + fresh
        weighted_ref[...] = weighted_ref[...] + fresh * intensity
        plane = (step * len(skewed) + g).astype(jnp.float32)
        depth_value = (plane + 0.5) / jnp.asarray(len(skewed) * pl.num_programs(0), jnp.float32)
        placed_ref[...] = placed_ref[...] + fresh * depth_value

    @pl.when(step == pl.num_programs(0) - 1)
    def _():
        rows, cols = joined_ref.shape
        top, left = crop

        def cropped(values):
            return pltpu.roll(values, width - left, 1)[top : top + rows, :cols]

        joined_ref[...] = cropped(weighted_ref[...] / total_ref[...])
        mean_ref[...] = cropped(placed_ref[...] / total_ref[...])


def propagate(taps, window, n_out, first_row):
    planes = taps.shape[0]
    _, window_rows, width = window.shape
    n_in = n_out + TAPS
    block_count = width // LANE - 1
    stacked = window.reshape(2 * window_rows, width)
    body = functools.partial(
        propagate_kernel, n_out=n_out, n_in=n_in, block_count=block_count,
        starts=(first_row, window_rows + first_row),
    )
    flops = 2 * planes * (2 * n_out * 2 * n_in * width + block_count * n_out * 4 * LANE * SPAN)
    return pl.pallas_call(
        body,
        grid=(planes,),
        in_specs=[
            pl.BlockSpec((1, 2, SPAN), lambda p: (p, 0, 0)),
            pl.BlockSpec((2 * window_rows, width), lambda p: (0, 0)),
        ],
        out_specs=pl.BlockSpec((1, n_out, block_count * LANE), lambda p: (p, 0, 0)),
        out_shape=jax.ShapeDtypeStruct((planes, n_out, block_count * LANE), jnp.float32),
        cost_estimate=pl.CostEstimate(
            flops=flops,
            transcendentals=0,
            bytes_accessed=stacked.size * 2 + planes * n_out * block_count * LANE * 4,
        ),
    )(taps, stacked)


def joining(corner, taps, prior, window, n_out, first_row, bounds, crop, out_shape):
    planes = taps.shape[0]
    group = 32 if planes % 32 == 0 else planes
    _, window_rows, width = window.shape
    n_in = SPAN
    block_count = width // LANE - 1
    stacked = window.reshape(2 * window_rows, width)
    body = functools.partial(
        joining_kernel, n_out=n_out, n_in=n_in, block_count=block_count, bounds=bounds,
        crop=crop, starts=(first_row, window_rows + first_row),
    )
    out_cols = block_count * LANE
    flops = 2 * planes * (2 * n_out * 2 * n_in * width + block_count * n_out * 4 * LANE * SPAN)
    grid_spec = pltpu.PrefetchScalarGridSpec(
        num_scalar_prefetch=1,
        grid=(planes // group,),
        in_specs=[
            pl.BlockSpec((group, taps.shape[1]), lambda p, c: (p, 0)),
            pl.BlockSpec((group, n_out, LANE), lambda p, c: (p, 0, 0)),
            pl.BlockSpec((2 * window_rows, width), lambda p, c: (0, 0)),
        ],
        out_specs=[
            pl.BlockSpec(out_shape, lambda p, c: (0, 0)),
            pl.BlockSpec(out_shape, lambda p, c: (0, 0)),
        ],
        scratch_shapes=[pltpu.VMEM((n_out, out_cols), jnp.float32) for _ in range(3)],
    )
    return pl.pallas_call(
        body,
        grid_spec=grid_spec,
        out_shape=[jax.ShapeDtypeStruct(out_shape, jnp.float32)] * 2,
        compiler_params=pltpu.CompilerParams(dimension_semantics=("arbitrary",)),
        cost_estimate=pl.CostEstimate(
            flops=flops,
            transcendentals=0,
            bytes_accessed=stacked.size * 2 + 2 * n_out * out_cols * 4,
        ),
    )(corner, taps, prior, stacked)


def gather_depth(block):
    count = lax.axis_size("depth")
    copies = jnp.broadcast_to(block[None], (count,) + block.shape)
    moved = lax.all_to_all(copies, "depth", 0, 0)
    return moved.reshape(count * block.shape[0], block.shape[1])


def local(hologram, kernel, depth_prior):
    _, rows, col_total = hologram.shape
    local_planes = kernel.shape[0]
    depth_count = lax.axis_size("depth")
    tile_count = lax.axis_size("tile")
    depth_at = lax.axis_index("depth")
    tile_at = lax.axis_index("tile")
    planes_total = local_planes * depth_count
    own_cols = col_total // depth_count
    row_total = rows * tile_count
    half_taps = TAPS // 2

    taps = jnp.pad(kernel.astype(jnp.float32), ((0, 0), (0, 0), (0, SPAN - TAPS)))
    packed = jnp.concatenate([taps.reshape(local_planes, 2 * SPAN), depth_prior], axis=1)
    packed_all = gather_depth(packed)

    halo = 48
    above = lax.ppermute(hologram, "tile", [(i, i + 1) for i in range(tile_count - 1)])
    below = lax.ppermute(hologram, "tile", [(i + 1, i) for i in range(tile_count - 1)])
    extended = jnp.concatenate([above[:, rows - halo :], hologram, below[:, :halo]], axis=1)
    extended = jnp.pad(extended, ((0, 0), (0, 0), (half_taps, LANE - half_taps)))

    plane_stack = propagate(taps, extended, rows, halo - half_taps)
    plane_stack, packed_all = lax.optimization_barrier((plane_stack, packed_all))
    prior_all = packed_all[:, 2 * SPAN :]

    lead_rows = 8
    n_out = rows + 2 * lead_rows
    first = halo - half_taps - lead_rows
    lead = LANE // 2
    width = own_cols + 2 * LANE
    window = jnp.pad(extended, ((0, 0), (0, first + SPAN - extended.shape[1]), (lead, lead)))
    window = lax.dynamic_slice_in_dim(window, depth_at * own_cols, width, axis=2)
    corner = jnp.stack([tile_at * rows - lead_rows, depth_at * own_cols - LANE // 2]).astype(
        jnp.int32
    )
    prior_weight = jnp.exp(prior_all - jnp.max(prior_all, axis=0, keepdims=True))
    prior_rows = jnp.pad(prior_weight, ((0, 0), (lead_rows, lead_rows)), constant_values=1.0)
    joined, mean_depth = joining(
        corner, packed_all, jnp.broadcast_to(prior_rows[:, :, None], prior_rows.shape + (LANE,)),
        window, n_out, first,
        (row_total, col_total), (lead_rows, LANE // 2), (rows, own_cols),
    )
    return (plane_stack, joined, mean_depth)


def solution(mesh):
    in_specs = (P(None, "tile", None), P("depth", None, None), P("depth", "tile"))
    out_specs = (P("depth", "tile", None), P("tile", "depth"), P("tile", "depth"))
    return jax.shard_map(local, mesh=mesh, in_specs=in_specs, out_specs=out_specs, check_vma=False)
```

```python
import functools

import jax
import jax.numpy as jnp
from jax import lax
from jax.experimental import pallas as pl
from jax.experimental.pallas import tpu as pltpu
from jax.sharding import PartitionSpec as P

TAPS = 64
LANE = 128
SPAN = 2 * LANE


def skews(taps_ref, plane):
    def skew(taps):
        return pltpu.roll(jnp.broadcast_to(taps, (LANE, SPAN)), 0, 1, stride=1, stride_axis=0)

    if len(taps_ref.shape) == 3:
        return skew(taps_ref[plane, 0:1, :]), skew(taps_ref[plane, 1:2, :])
    row = taps_ref[plane : plane + 1]
    return skew(row[:, :SPAN]), skew(row[:, SPAN : 2 * SPAN])


def rows_matrix(skew_re, skew_im, n_out, n_in):
    rows_re = skew_re[:n_out, :n_in]
    rows_im = skew_im[:n_out, :n_in]
    return jnp.concatenate(
        [
            jnp.concatenate([rows_re, -rows_im], axis=1),
            jnp.concatenate([rows_im, rows_re], axis=1),
        ],
        axis=0,
    ).astype(jnp.bfloat16)


def across_planes(taps_ref, window_ref, n_out, n_in, starts):
    group = taps_ref.shape[0]
    skewed = [skews(taps_ref, g) for g in range(group)]
    matrix = jnp.concatenate([rows_matrix(*sk, n_out, n_in) for sk in skewed], axis=0)
    across = jnp.dot(
        matrix[:, :n_in], window_ref[starts[0] : starts[0] + n_in], preferred_element_type=jnp.float32
    ) + jnp.dot(
        matrix[:, n_in:], window_ref[starts[1] : starts[1] + n_in], preferred_element_type=jnp.float32
    )
    return skewed, across.astype(jnp.bfloat16)


def column_intensity(across, skew_re, skew_im, n_out, block_count):
    across_re = across[:n_out]
    across_im = across[n_out:]

    def stacked(signal, first):
        return jnp.concatenate(
            [signal[:, LANE * b : LANE * (b + 1)] for b in range(first, first + block_count)], axis=0
        )

    blocks = jnp.concatenate(
        [stacked(across_re, 0), stacked(across_re, 1), stacked(across_im, 0), stacked(across_im, 1)],
        axis=1,
    )
    near_re = skew_re[:, :LANE].T
    far_re = skew_re[:, LANE:].T
    near_im = skew_im[:, :LANE].T
    far_im = skew_im[:, LANE:].T
    cols_matrix = jnp.concatenate(
        [
            jnp.concatenate([near_re, near_im], axis=1),
            jnp.concatenate([far_re, far_im], axis=1),
            jnp.concatenate([-near_im, near_re], axis=1),
            jnp.concatenate([-far_im, far_re], axis=1),
        ],
        axis=0,
    ).astype(jnp.bfloat16)
    field = jnp.dot(blocks, cols_matrix, preferred_element_type=jnp.float32)
    return field[:, :LANE] * field[:, :LANE] + field[:, LANE:] * field[:, LANE:]


def propagate_kernel(taps_ref, window_ref, out_ref, *, n_out, n_in, block_count, starts):
    skewed, across = across_planes(taps_ref, window_ref, n_out, n_in, starts)
    for g, (skew_re, skew_im) in enumerate(skewed):
        intensity = column_intensity(
            across[2 * n_out * g : 2 * n_out * (g + 1)], skew_re, skew_im, n_out, block_count
        )
        for b in range(block_count):
            out_ref[g, :, LANE * b : LANE * (b + 1)] = intensity[n_out * b : n_out * (b + 1)]


def joining_kernel(
    corner_ref, taps_ref, prior_ref, depth_ref, window_ref, joined_ref, mean_ref,
    total_ref, weighted_ref, placed_ref, *, n_out, n_in, block_count, bounds, crop, starts,
):
    step = pl.program_id(0)

    @pl.when(step == 0)
    def _():
        total_ref[...] = jnp.zeros(total_ref.shape, jnp.float32)
        weighted_ref[...] = jnp.zeros(weighted_ref.shape, jnp.float32)
        placed_ref[...] = jnp.zeros(placed_ref.shape, jnp.float32)

    skewed, across = across_planes(taps_ref, window_ref, n_out, n_in, starts)
    height, width = n_out, block_count * LANE
    row_at = corner_ref[0] + lax.broadcasted_iota(jnp.int32, (height, width), 0)
    col_at = corner_ref[1] + lax.broadcasted_iota(jnp.int32, (height, width), 1)
    inside = (row_at >= 0) & (row_at < bounds[0]) & (col_at >= 0) & (col_at < bounds[1])
    for g, (skew_re, skew_im) in enumerate(skewed):
        stacked = column_intensity(
            across[2 * n_out * g : 2 * n_out * (g + 1)], skew_re, skew_im, n_out, block_count
        )
        intensity = jnp.concatenate(
            [stacked[n_out * b : n_out * (b + 1)] for b in range(block_count)], axis=1
        )
        intensity = jnp.where(inside, intensity, 0.0)
        vertical = (
            pltpu.roll(intensity, 1, 0) + 2.0 * intensity + pltpu.roll(intensity, height - 1, 0)
        )
        grad_x = pltpu.roll(vertical, width - 1, 1) - pltpu.roll(vertical, 1, 1)
        horizontal = (
            pltpu.roll(intensity, 1, 1) + 2.0 * intensity + pltpu.roll(intensity, width - 1, 1)
        )
        grad_y = pltpu.roll(horizontal, height - 1, 0) - pltpu.roll(horizontal, 1, 0)
        fresh = prior_ref[g][:, 0:1] * (1.0 + (grad_x * grad_x + grad_y * grad_y))
        total_ref[...] = total_ref[...] + fresh
        weighted_ref[...] = weighted_ref[...] + fresh * intensity
        placed_ref[...] = placed_ref[...] + fresh * depth_ref[g]

    @pl.when(step == pl.num_programs(0) - 1)
    def _():
        rows, cols = joined_ref.shape
        top, left = crop

        def cropped(values):
            return pltpu.roll(values, width - left, 1)[top : top + rows, :cols]

        joined_ref[...] = cropped(weighted_ref[...] / total_ref[...])
        mean_ref[...] = cropped(placed_ref[...] / total_ref[...])


def propagate(taps, window, n_out, first_row):
    planes = taps.shape[0]
    pair = 2 if planes % 2 == 0 else 1
    _, window_rows, width = window.shape
    n_in = n_out + TAPS
    block_count = width // LANE - 1
    stacked = window.reshape(2 * window_rows, width)
    body = functools.partial(
        propagate_kernel, n_out=n_out, n_in=n_in, block_count=block_count,
        starts=(first_row, window_rows + first_row),
    )
    flops = 2 * planes * (2 * n_out * 2 * n_in * width + block_count * n_out * 4 * LANE * SPAN)
    return pl.pallas_call(
        body,
        grid=(planes // pair,),
        in_specs=[
            pl.BlockSpec((pair, 2, SPAN), lambda p: (p, 0, 0)),
            pl.BlockSpec((2 * window_rows, width), lambda p: (0, 0)),
        ],
        out_specs=pl.BlockSpec((pair, n_out, block_count * LANE), lambda p: (p, 0, 0)),
        out_shape=jax.ShapeDtypeStruct((planes, n_out, block_count * LANE), jnp.float32),
        cost_estimate=pl.CostEstimate(
            flops=flops,
            transcendentals=0,
            bytes_accessed=stacked.size * 2 + planes * n_out * block_count * LANE * 4,
        ),
    )(taps, stacked)


def joining(corner, taps, prior, depth_values, window, n_out, first_row, bounds, crop, out_shape):
    planes = taps.shape[0]
    group = 32 if planes % 32 == 0 else planes
    _, window_rows, width = window.shape
    n_in = SPAN
    block_count = width // LANE - 1
    stacked = window.reshape(2 * window_rows, width)
    body = functools.partial(
        joining_kernel, n_out=n_out, n_in=n_in, block_count=block_count, bounds=bounds,
        crop=crop, starts=(first_row, window_rows + first_row),
    )
    out_cols = block_count * LANE
    flops = 2 * planes * (2 * n_out * 2 * n_in * width + block_count * n_out * 4 * LANE * SPAN)
    grid_spec = pltpu.PrefetchScalarGridSpec(
        num_scalar_prefetch=1,
        grid=(planes // group,),
        in_specs=[
            pl.BlockSpec((group, taps.shape[1]), lambda p, c: (p, 0)),
            pl.BlockSpec((group, n_out, LANE), lambda p, c: (p, 0, 0)),
            pl.BlockSpec((group, 1, 1), lambda p, c: (p, 0, 0)),
            pl.BlockSpec((2 * window_rows, width), lambda p, c: (0, 0)),
        ],
        out_specs=[
            pl.BlockSpec(out_shape, lambda p, c: (0, 0)),
            pl.BlockSpec(out_shape, lambda p, c: (0, 0)),
        ],
        scratch_shapes=[pltpu.VMEM((n_out, out_cols), jnp.float32) for _ in range(3)],
    )
    return pl.pallas_call(
        body,
        grid_spec=grid_spec,
        out_shape=[jax.ShapeDtypeStruct(out_shape, jnp.float32)] * 2,
        compiler_params=pltpu.CompilerParams(dimension_semantics=("arbitrary",)),
        cost_estimate=pl.CostEstimate(
            flops=flops,
            transcendentals=0,
            bytes_accessed=stacked.size * 2 + 2 * n_out * out_cols * 4,
        ),
    )(corner, taps, prior, depth_values, stacked)


def gather_depth(block):
    count = lax.axis_size("depth")
    copies = jnp.broadcast_to(block[None], (count,) + block.shape)
    moved = lax.all_to_all(copies, "depth", 0, 0)
    return moved.reshape(count * block.shape[0], block.shape[1])


def local(hologram, kernel, depth_prior):
    _, rows, col_total = hologram.shape
    local_planes = kernel.shape[0]
    depth_count = lax.axis_size("depth")
    tile_count = lax.axis_size("tile")
    depth_at = lax.axis_index("depth")
    tile_at = lax.axis_index("tile")
    planes_total = local_planes * depth_count
    own_cols = col_total // depth_count
    row_total = rows * tile_count
    half_taps = TAPS // 2

    taps = jnp.pad(kernel.astype(jnp.float32), ((0, 0), (0, 0), (0, SPAN - TAPS)))
    packed = jnp.concatenate([taps.reshape(local_planes, 2 * SPAN), depth_prior], axis=1)
    packed_all = gather_depth(packed)
    plane_at = jnp.arange(planes_total)

    halo = 48
    above = lax.ppermute(hologram, "tile", [(i, i + 1) for i in range(tile_count - 1)])
    below = lax.ppermute(hologram, "tile", [(i + 1, i) for i in range(tile_count - 1)])
    extended = jnp.concatenate([above[:, rows - halo :], hologram, below[:, :halo]], axis=1)
    extended = jnp.pad(extended, ((0, 0), (0, 0), (half_taps, LANE - half_taps)))

    plane_stack = propagate(taps, extended, rows, halo - half_taps)
    plane_stack, packed_all = lax.optimization_barrier((plane_stack, packed_all))
    prior_all = packed_all[:, 2 * SPAN :]

    lead_rows = 8
    n_out = rows + 2 * lead_rows
    first = halo - half_taps - lead_rows
    lead = LANE // 2
    width = own_cols + 2 * LANE
    window = jnp.pad(extended, ((0, 0), (0, first + SPAN - extended.shape[1]), (lead, lead)))
    window = lax.dynamic_slice_in_dim(window, depth_at * own_cols, width, axis=2)
    corner = jnp.stack([tile_at * rows - lead_rows, depth_at * own_cols - LANE // 2]).astype(
        jnp.int32
    )
    prior_weight = jnp.exp(prior_all - jnp.max(prior_all, axis=0, keepdims=True))
    prior_rows = jnp.pad(prior_weight, ((0, 0), (lead_rows, lead_rows)), constant_values=1.0)
    depth_values = ((plane_at.astype(jnp.float32) + 0.5) / planes_total)[:, None, None]
    joined, mean_depth = joining(
        corner, packed_all, jnp.broadcast_to(prior_rows[:, :, None], prior_rows.shape + (LANE,)),
        depth_values, window, n_out, first,
        (row_total, col_total), (lead_rows, LANE // 2), (rows, own_cols),
    )
    return (plane_stack, joined, mean_depth)


def solution(mesh):
    in_specs = (P(None, "tile", None), P("depth", None, None), P("depth", "tile"))
    out_specs = (P("depth", "tile", None), P("tile", "depth"), P("tile", "depth"))
    return jax.shard_map(local, mesh=mesh, in_specs=in_specs, out_specs=out_specs, check_vma=False)
```
